512 devices in a mesh: pipe: 32 (over y, z_lo), seq: 16 (over z_hi, x, core).
Axes of the slice: x: 4, y: 8, z: 8 (z_hi: 2, z_lo: 4; z = z_hi * 4 + z_lo), core: 2. Of those that a mesh axis runs over, the one named last changes fastest.
Arguments:
- x_first: bfloat16 [4096, 2560], P(('pipe', 'seq')), may hold values from -6 to 6
- x_second: bfloat16 [4096, 2560], P(('pipe', 'seq')), may hold values from -6 to 6
- stale_kv: bfloat16 [2, 4096, 2048], P(None, 'pipe', 'seq'), may hold values from -6 to 6
- w_qkv: bfloat16 [3, 2560, 2048], P(None, None, 'seq'), may hold values from -0.125 to 0.125
- w_out: bfloat16 [2048, 2560], P('seq'), may hold values from -0.125 to 0.125
- q_gain: float32 [2048], P('seq'), may hold values from 0.4 to 5
- k_gain: float32 [2048], P('seq'), may hold values from 0.4 to 5
- layout: int32 [32, 16], replicated, may hold values from 0 to 31, as said below
- counts: int32 [32], replicated, may hold values from 1 to 16, as said below
- slot_block: int32 [32], replicated, may hold values from 0 to 31, each once
Outputs:
- out_first: bfloat16 [4096, 2560], P(('pipe', 'seq'))
- out_second: bfloat16 [4096, 2560], P(('pipe', 'seq'))
The draws below stay inside these ranges and needn't reach their ends.
Inputs may be any that keep to these rules, and one draw needn't show every extreme that they name: `layout`: entries of a row are distinct sequence blocks and the first entry of row b is b itself. `counts`: some block reads 16 entries. `slot_block`: each block once.
All inputs are finite; a program needn't handle non-finite values.
Results may differ from the reference program's by a relative error of at most 0.019.
Values may be sent and summed in bfloat16 or wider, within the bound.
No kernel may reach another device: no remote copies, remote signals or barrier semaphores. Data moves between devices by JAX's collectives and lax.ppermute only.
A program may use at most 64 MiB of HBM per device.

```python
import math
import jax
import jax.numpy as jnp
from jax import lax

D = 2560
HS = 64
HEADS = 32
BLOCK = 128
NK = 16
BPM = 1
NB = 32
SEQ = 4096
N_PIPE = 32
N_SEQ = 16


def layout_pair(key):
    cols = jnp.arange(NB, dtype=jnp.int32)
    scores = jax.random.randint(jax.random.fold_in(key, 11), (NB, NB), 0, 2 ** 20)
    scores = scores * NB + cols[None, :]
    scores = jnp.where(cols[None, :] == cols[:, None], 2 ** 30, scores)
    listed = lax.top_k(scores, NK)[1].astype(jnp.int32)
    drawn = jax.random.randint(jax.random.fold_in(key, 12), (NB,), 1, NK + 1)
    drawn = jnp.where(cols == 0, NK, drawn).astype(jnp.int32)
    return (listed, drawn)


def draw_layout(key, part):
    return layout_pair(key)[0]


def draw_counts(key, part):
    return layout_pair(key)[1]


def gain_draw(key):
    spread = jax.random.uniform(jax.random.fold_in(key, 1), (HEADS * HS,), minval=math.log(0.5), maxval=math.log(2.0))
    return jnp.exp(spread).astype(jnp.float32)


def draw_q_gain(key, part):
    return gain_draw(jax.random.fold_in(key, 21))


def draw_k_gain(key, part):
    return gain_draw(jax.random.fold_in(key, 22))


def levels(key, dims, split, low, top_value):
    factor_of = 1.0
    for position, blocks in split:
        draws = jax.random.uniform(jax.random.fold_in(jax.random.fold_in(key, 6), position), (blocks,), jnp.float32, low / len(split), top_value / len(split))
        factor_of = factor_of * jnp.repeat(jnp.exp(draws), dims[position] // blocks).reshape((-1,) + (1,) * (len(dims) - 1 - position))
    return factor_of


def centred(rng, dims, deviation, limit, shards=(), kind=jnp.bfloat16):
    values = deviation * jax.random.normal(rng, dims, jnp.float32)
    if shards:
        values = values * levels(rng, dims, shards, -0.22, 0.18)
    return jnp.clip(values, -limit, limit).astype(kind)


def setup_inputs(seed: int = 0) -> dict:
    key_of = jax.random.split(jax.random.key(seed), 11)
    x_first = centred(key_of[0], (SEQ, D), 1.0, 6.0, ((0, 512),))
    x_second = centred(key_of[1], (SEQ, D), 1.0, 6.0, ((0, 512),))
    stale_kv = centred(key_of[2], (2, SEQ, HEADS * HS), 1.0, 6.0, ((1, 32), (2, 16)))
    w_qkv = centred(key_of[3], (3, D, HEADS * HS), D ** -0.5, 0.125, ((2, 16),))
    w_out = centred(key_of[4], (HEADS * HS, D), (HEADS * HS) ** -0.5, 0.125, ((0, 16),))
    q_gain = draw_q_gain(jax.random.fold_in(key_of[10], 71), 0)
    k_gain = draw_k_gain(jax.random.fold_in(key_of[10], 71), 0)
    layout = draw_layout(jax.random.fold_in(key_of[10], 71), 0)
    counts = draw_counts(jax.random.fold_in(key_of[10], 71), 0)
    slot_block = jax.random.permutation(key_of[9], NB).astype(jnp.int32)
    return dict(x_first=x_first, x_second=x_second, stale_kv=stale_kv, w_qkv=w_qkv, w_out=w_out, q_gain=q_gain, k_gain=k_gain, layout=layout, counts=counts, slot_block=slot_block)


HIGH = lax.Precision.HIGHEST
NEG = -1e+30

def slot_mask(layout, counts, slot_block):
    total = layout.shape[0]
    width = layout.shape[1]
    blocks = jnp.arange(total, dtype=jnp.int32)
    valid = jnp.arange(width, dtype=jnp.int32)[None, :] < counts[:, None]
    member = lax.optimization_barrier(jnp.sum(((layout[:, :, None] == blocks[None, None, :]) & valid[:, :, None]).astype(jnp.float32), axis=1))
    placed = (slot_block[:, None] == blocks[None, :]).astype(jnp.float32)
    linked = jnp.dot(jnp.dot(placed, member, precision=HIGH), placed.T, precision=HIGH)
    return linked > 0.5

def normalize(raw, gain, size):
    count = raw.shape[0]
    grid = raw.reshape(count, -1, size)
    factor = lax.rsqrt(lax.optimization_barrier(jnp.mean(grid * grid, axis=2, keepdims=True)) + 1e-06)
    return (grid * factor).reshape(count, -1) * gain[None, :]

def partial_attend(query, keys, values, allowed, scale):
    heads = query.shape[1]
    qrows = query.shape[0]
    krows = keys.shape[0]
    scores = jnp.einsum('qhd,khd->hqk', query.astype(jnp.float32), keys.astype(jnp.float32), precision=HIGH) * scale
    grid = scores.reshape(heads, qrows // BLOCK, BLOCK, krows // BLOCK, BLOCK)
    keep = allowed[None, :, None, :, None]
    grid = jnp.where(keep, grid, NEG)
    top = lax.optimization_barrier(jnp.max(grid, axis=(3, 4)))
    weights = jnp.where(keep, jnp.exp(grid - top[:, :, :, None, None]), 0.0)
    total = lax.optimization_barrier(jnp.sum(weights, axis=(3, 4)))
    weights = weights.reshape(heads, qrows, krows)
    summed = jnp.einsum('hqk,khd->qhd', weights, values.astype(jnp.float32), precision=HIGH)
    return (top.reshape(heads, qrows), total.reshape(heads, qrows), summed)

def reference(x_first, x_second, stale_kv, w_qkv, w_out, q_gain, k_gain, layout, counts, slot_block):
    linked = slot_mask(layout, counts, slot_block)
    scale = 1.0 / math.sqrt(HS)
    heads = HEADS
    tokens = BPM * BLOCK

    def project(x):
        raw = jnp.einsum('rd,cdh->crh', x.astype(jnp.float32), w_qkv.astype(jnp.float32), precision=HIGH)
        query = normalize(raw[0], q_gain, HS).astype(jnp.bfloat16)
        keys = normalize(raw[1], k_gain, HS).astype(jnp.bfloat16)
        values = raw[2].astype(jnp.bfloat16)
        return (query, keys, values)

    def step(x, prior_k, prior_v):
        query, keys, values = project(x)
        owner = jnp.arange(SEQ, dtype=jnp.int32) // tokens

        def per_batch(batch):
            rows = lax.dynamic_slice_in_dim(query, batch * tokens, tokens, 0)
            fresh = (owner == batch)[:, None]
            use_k = jnp.where(fresh, keys, prior_k)
            use_v = jnp.where(fresh, values, prior_v)
            cols = lax.dynamic_slice_in_dim(linked, batch * BPM, BPM, 0)
            top, total, summed = partial_attend(rows.reshape(tokens, heads, HS), use_k.reshape(SEQ, heads, HS), use_v.reshape(SEQ, heads, HS), cols, scale)
            return (summed / total.T[:, :, None]).reshape(tokens, heads * HS)
        attn = lax.map(per_batch, jnp.arange(N_PIPE, dtype=jnp.int32)).reshape(SEQ, heads * HS).astype(jnp.bfloat16)
        groups = attn.reshape(SEQ, N_SEQ, -1).transpose(1, 0, 2)
        weights = w_out.reshape(N_SEQ, -1, D)

        def add_group(acc, pair):
            part = jnp.dot(pair[0], pair[1], preferred_element_type=jnp.float32)
            part = lax.optimization_barrier(part.astype(jnp.bfloat16))
            return (acc + part.astype(jnp.float32), None)
        acc, unused = lax.scan(add_group, jnp.zeros((SEQ, D), jnp.float32), (groups, weights))
        return (acc.astype(jnp.bfloat16), keys, values)
    out_first, keys_first, values_first = step(x_first, stale_kv[0], stale_kv[1])
    out_second, unused_k, unused_v = step(x_second, keys_first, values_first)
    return (out_first, out_second)
```

```python
import math

import jax
import jax.numpy as jnp
import numpy as np
from jax import lax
from jax.sharding import Mesh
from jax.sharding import PartitionSpec as P

HS = 64
BLOCK = 128
BPM = 1


HIGH = lax.Precision.HIGHEST
NEG = -1e30

PIPE_PARTS = (("y", 8), ("zl", 4))
SEQ_PARTS = (("zh", 2), ("x", 4), ("c", 2))
PIPE = tuple(n for n, _ in PIPE_PARTS)
SEQ = tuple(n for n, _ in SEQ_PARTS)


def slot_mask(layout, counts, slot_block):
    total = layout.shape[0]
    width = layout.shape[1]
    blocks = jnp.arange(total, dtype=jnp.int32)
    valid = jnp.arange(width, dtype=jnp.int32)[None, :] < counts[:, None]
    member = jnp.sum(
        ((layout[:, :, None] == blocks[None, None, :]) & valid[:, :, None]).astype(jnp.float32),
        axis=1,
    )
    placed = (slot_block[:, None] == blocks[None, :]).astype(jnp.float32)
    linked = jnp.dot(jnp.dot(placed, member, precision=HIGH), placed.T, precision=HIGH)
    return linked > 0.5


def normalize(raw, gain, size):
    count = raw.shape[0]
    grid = raw.reshape(count, -1, size)
    factor = lax.rsqrt(jnp.mean(grid * grid, axis=2, keepdims=True) + 1e-06)
    return (grid * factor).reshape(count, -1) * gain[None, :]


def partial_attend(query, keys, values, allowed, scale):
    heads = query.shape[1]
    qrows = query.shape[0]
    krows = keys.shape[0]
    scores = jnp.einsum("qhd,khd->hqk", query, keys, preferred_element_type=jnp.float32) * scale
    grid = scores.reshape(heads, qrows // BLOCK, BLOCK, krows // BLOCK, BLOCK)
    keep = allowed[None, :, None, :, None]
    grid = jnp.where(keep, grid, NEG)
    top = jnp.max(grid, axis=(3, 4))
    weights = jnp.where(keep, jnp.exp(grid - top[:, :, :, None, None]), 0.0)
    total = jnp.sum(weights, axis=(3, 4))
    weights = weights.reshape(heads, qrows, krows)
    summed = jnp.einsum("hqk,khd->qhd", weights, values.astype(jnp.float32), precision=HIGH)
    return (top.reshape(heads, qrows), total.reshape(heads, qrows), summed)


def merge_parts(first, second):
    top_a, total_a, summed_a = first
    top_b, total_b, summed_b = second
    best = jnp.maximum(top_a, top_b)
    keep_a = jnp.exp(top_a - best)
    keep_b = jnp.exp(top_b - best)
    merged = summed_a * keep_a.T[:, :, None] + summed_b * keep_b.T[:, :, None]
    return (best, total_a * keep_a + total_b * keep_b, merged)


def gather_pipe(piece):
    for name in reversed(PIPE):
        piece = lax.all_gather(piece, name, axis=0, tiled=True)
    return piece


def on_device(
    x_first, x_second, stale_kv, w_qkv, w_out, q_gain, k_gain, layout, counts, slot_block
):
    me = lax.axis_index(PIPE)
    n_seq = math.prod(s for _, s in SEQ_PARTS)
    tokens = BPM * BLOCK
    heads = w_qkv.shape[2] // HS
    width = heads * HS
    scale = 1.0 / math.sqrt(HS)
    linked = slot_mask(layout, counts, slot_block)
    total_blocks = linked.shape[0]
    block_ids = jnp.arange(total_blocks, dtype=jnp.int32)
    batch_of = block_ids // BPM
    mine = lax.dynamic_slice_in_dim(linked, me * BPM, BPM, 0)
    own = lax.dynamic_slice_in_dim(mine, me * BPM, BPM, 1)
    remote = mine & (batch_of != me)[None, :]

    xs = lax.all_gather(jnp.stack([x_first, x_second]), SEQ, axis=1, tiled=True)

    def project(x):
        raw = jnp.einsum("rd,cdh->crh", x, w_qkv, preferred_element_type=jnp.float32)
        query = normalize(raw[0], q_gain, HS).astype(jnp.bfloat16)
        keys = normalize(raw[1], k_gain, HS).astype(jnp.bfloat16)
        values = raw[2].astype(jnp.bfloat16)
        return (query, keys, values)

    q1, k1, v1 = project(xs[0])
    q2, k2, v2 = project(xs[1])

    kv = jnp.stack([stale_kv[0], stale_kv[1], k1, v1])[None]
    gathered = gather_pipe(kv)
    count = gathered.shape[0] * tokens

    def attend(query, keys, values, piece_k, piece_v):
        query_h = query.reshape(tokens, heads, HS)
        start_part = partial_attend(
            query_h, keys.reshape(tokens, heads, HS), values.reshape(tokens, heads, HS), own, scale
        )
        fresh = partial_attend(
            query_h,
            piece_k.reshape(count, heads, HS),
            piece_v.reshape(count, heads, HS),
            remote,
            scale,
        )
        best, denom_h, numer = merge_parts(start_part, fresh)
        denom = denom_h.T
        attn = (numer / denom[:, :, None]).reshape(tokens, width).astype(jnp.bfloat16)
        return jnp.dot(attn, w_out, preferred_element_type=jnp.float32).astype(jnp.bfloat16)

    part1 = attend(q1, k1, v1, gathered[:, 0], gathered[:, 1])
    part2 = attend(q2, k2, v2, gathered[:, 2], gathered[:, 3])
    parts = jnp.stack([part1, part2])
    sent = lax.all_to_all(
        parts.reshape(2, n_seq, tokens // n_seq, -1), SEQ, 1, 1, tiled=False
    )
    out = jnp.sum(sent.astype(jnp.float32), axis=1).astype(jnp.bfloat16)
    return (out[0], out[1])


def solution(mesh):
    names = PIPE_PARTS + SEQ_PARTS
    fine = Mesh(
        np.asarray(mesh.devices).reshape([s for _, s in names]), tuple(n for n, _ in names)
    )
    rows = P(PIPE + SEQ, None)
    placed = (
        rows,
        rows,
        P(None, PIPE, SEQ),
        P(None, None, SEQ),
        P(SEQ, None),
        P(SEQ),
        P(SEQ),
        P(),
        P(),
        P(),
    )
    return jax.shard_map(
        on_device,
        mesh=fine,
        in_specs=placed,
        out_specs=(rows, rows),
        check_vma=False,
    )
```

```python
import math

import jax
import jax.numpy as jnp
import numpy as np
from jax import lax
from jax.sharding import Mesh
from jax.sharding import PartitionSpec as P

HS = 64
BLOCK = 128
BPM = 1


HIGH = lax.Precision.HIGHEST
NEG = -1e30

PIPE_PARTS = (("y", 8), ("zl", 4))
SEQ_PARTS = (("zh", 2), ("x", 4), ("c", 2))
PIPE = tuple(n for n, _ in PIPE_PARTS)
SEQ = tuple(n for n, _ in SEQ_PARTS)


def slot_mask(layout, counts, slot_block):
    total = layout.shape[0]
    width = layout.shape[1]
    blocks = jnp.arange(total, dtype=jnp.int32)
    valid = jnp.arange(width, dtype=jnp.int32)[None, :] < counts[:, None]
    member = jnp.sum(
        ((layout[:, :, None] == blocks[None, None, :]) & valid[:, :, None]).astype(jnp.float32),
        axis=1,
    )
    placed = (slot_block[:, None] == blocks[None, :]).astype(jnp.float32)
    linked = jnp.dot(jnp.dot(placed, member, precision=HIGH), placed.T, precision=HIGH)
    return linked > 0.5


def normalize(raw, gain, size):
    count = raw.shape[0]
    grid = raw.reshape(count, -1, size)
    factor = lax.rsqrt(jnp.mean(grid * grid, axis=2, keepdims=True) + 1e-06)
    return (grid * factor).reshape(count, -1) * gain[None, :]


def partial_attend(query, keys, values, allowed, scale):
    heads = query.shape[1]
    qrows = query.shape[0]
    krows = keys.shape[0]
    scores = jnp.einsum("qhd,khd->hqk", query, keys, preferred_element_type=jnp.float32) * scale
    grid = scores.reshape(heads, qrows // BLOCK, BLOCK, krows // BLOCK, BLOCK)
    keep = allowed[None, :, None, :, None]
    grid = jnp.where(keep, grid, NEG)
    top = jnp.max(grid, axis=(3, 4))
    weights = jnp.where(keep, jnp.exp(grid - top[:, :, :, None, None]), 0.0)
    total = jnp.sum(weights, axis=(3, 4))
    weights = weights.reshape(heads, qrows, krows)
    summed = jnp.einsum("hqk,khd->qhd", weights, values.astype(jnp.float32), precision=HIGH)
    return (top.reshape(heads, qrows), total.reshape(heads, qrows), summed)


def merge_parts(first, second):
    top_a, total_a, summed_a = first
    top_b, total_b, summed_b = second
    best = jnp.maximum(top_a, top_b)
    keep_a = jnp.exp(top_a - best)
    keep_b = jnp.exp(top_b - best)
    merged = summed_a * keep_a.T[:, :, None] + summed_b * keep_b.T[:, :, None]
    return (best, total_a * keep_a + total_b * keep_b, merged)


def gather_pipe(piece):
    for name in reversed(PIPE):
        piece = lax.all_gather(piece, name, axis=0, tiled=True)
    return piece


def on_device(
    x_first, x_second, stale_kv, w_qkv, w_out, q_gain, k_gain, layout, counts, slot_block
):
    me = lax.axis_index(PIPE)
    n_seq = math.prod(s for _, s in SEQ_PARTS)
    tokens = BPM * BLOCK
    heads = w_qkv.shape[2] // HS
    width = heads * HS
    scale = 1.0 / math.sqrt(HS)
    linked = slot_mask(layout, counts, slot_block)
    total_blocks = linked.shape[0]
    block_ids = jnp.arange(total_blocks, dtype=jnp.int32)
    batch_of = block_ids // BPM
    mine = lax.dynamic_slice_in_dim(linked, me * BPM, BPM, 0)
    own = lax.dynamic_slice_in_dim(mine, me * BPM, BPM, 1)
    remote = mine & (batch_of != me)[None, :]

    stale = gather_pipe(stale_kv[None])

    pair = jnp.stack([x_first, x_second])
    spread = jnp.broadcast_to(pair[:, None], (2, n_seq) + x_first.shape)
    xs = lax.all_to_all(spread, SEQ, 1, 1, tiled=False).reshape(2, tokens, -1)

    def project(x):
        raw = jnp.einsum("rd,cdh->crh", x, w_qkv, preferred_element_type=jnp.float32)
        query = normalize(raw[0], q_gain, HS).astype(jnp.bfloat16)
        keys = normalize(raw[1], k_gain, HS).astype(jnp.bfloat16)
        values = raw[2].astype(jnp.bfloat16)
        return (query, keys, values)

    q1, k1, v1 = project(xs[0])
    q2, k2, v2 = project(xs[1])

    fresh_kv = gather_pipe(jnp.stack([k1, v1])[None])
    count = fresh_kv.shape[0] * tokens

    def attend(query, keys, values, piece_k, piece_v):
        query_h = query.reshape(tokens, heads, HS)
        start_part = partial_attend(
            query_h, keys.reshape(tokens, heads, HS), values.reshape(tokens, heads, HS), own, scale
        )
        fresh = partial_attend(
            query_h,
            piece_k.reshape(count, heads, HS),
            piece_v.reshape(count, heads, HS),
            remote,
            scale,
        )
        best, denom_h, numer = merge_parts(start_part, fresh)
        denom = denom_h.T
        attn = (numer / denom[:, :, None]).reshape(tokens, width).astype(jnp.bfloat16)
        part = jnp.dot(attn, w_out, preferred_element_type=jnp.float32).astype(jnp.bfloat16)
        sent = lax.all_to_all(part.reshape(n_seq, tokens // n_seq, -1), SEQ, 0, 0, tiled=False)
        return jnp.sum(sent.astype(jnp.float32), axis=0).astype(jnp.bfloat16)

    out_first = attend(q1, k1, v1, stale[:, 0], stale[:, 1])
    out_first, fresh_kv = lax.optimization_barrier((out_first, fresh_kv))
    out_second = attend(q2, k2, v2, fresh_kv[:, 0], fresh_kv[:, 1])
    return (out_first, out_second)


def solution(mesh):
    names = PIPE_PARTS + SEQ_PARTS
    fine = Mesh(
        np.asarray(mesh.devices).reshape([s for _, s in names]), tuple(n for n, _ in names)
    )
    rows = P(PIPE + SEQ, None)
    placed = (
        rows,
        rows,
        P(None, PIPE, SEQ),
        P(None, None, SEQ),
        P(SEQ, None),
        P(SEQ),
        P(SEQ),
        P(),
        P(),
        P(),
    )
    return jax.shard_map(
        on_device,
        mesh=fine,
        in_specs=placed,
        out_specs=(rows, rows),
        check_vma=False,
    )
```

```python
import math

import jax
import jax.numpy as jnp
import numpy as np
from jax import lax
from jax.sharding import Mesh
from jax.sharding import PartitionSpec as P

HS = 64
BLOCK = 128
BPM = 1


HIGH = lax.Precision.HIGHEST
NEG = -1e30

PIPE_PARTS = (("y", 8), ("zl", 4))
SEQ_PARTS = (("zh", 2), ("x", 4), ("c", 2))
PIPE = tuple(n for n, _ in PIPE_PARTS)
SEQ = tuple(n for n, _ in SEQ_PARTS)


def slot_mask(layout, counts, slot_block):
    total = layout.shape[0]
    width = layout.shape[1]
    blocks = jnp.arange(total, dtype=jnp.int32)
    valid = jnp.arange(width, dtype=jnp.int32)[None, :] < counts[:, None]
    member = jnp.sum(
        ((layout[:, :, None] == blocks[None, None, :]) & valid[:, :, None]).astype(jnp.float32),
        axis=1,
    )
    placed = (slot_block[:, None] == blocks[None, :]).astype(jnp.float32)
    linked = jnp.dot(jnp.dot(placed, member, precision=HIGH), placed.T, precision=HIGH)
    return linked > 0.5


def normalize(raw, gain, size):
    count = raw.shape[0]
    grid = raw.reshape(count, -1, size)
    factor = lax.rsqrt(jnp.mean(grid * grid, axis=2, keepdims=True) + 1e-06)
    return (grid * factor).reshape(count, -1) * gain[None, :]


def partial_attend(query, keys, values, allowed, scale):
    heads = query.shape[1]
    qrows = query.shape[0]
    krows = keys.shape[0]
    scores = jnp.einsum("qhd,khd->hqk", query, keys, preferred_element_type=jnp.float32) * scale
    grid = scores.reshape(heads, qrows // BLOCK, BLOCK, krows // BLOCK, BLOCK)
    keep = allowed[None, :, None, :, None]
    grid = jnp.where(keep, grid, NEG)
    top = jnp.max(grid, axis=(3, 4))
    weights = jnp.where(keep, jnp.exp(grid - top[:, :, :, None, None]), 0.0)
    total = jnp.sum(weights, axis=(3, 4))
    weights = weights.reshape(heads, qrows, krows)
    summed = jnp.einsum("hqk,khd->qhd", weights, values.astype(jnp.float32), precision=HIGH)
    return (top.reshape(heads, qrows), total.reshape(heads, qrows), summed)


def merge_parts(first, second):
    top_a, total_a, summed_a = first
    top_b, total_b, summed_b = second
    best = jnp.maximum(top_a, top_b)
    keep_a = jnp.exp(top_a - best)
    keep_b = jnp.exp(top_b - best)
    merged = summed_a * keep_a.T[:, :, None] + summed_b * keep_b.T[:, :, None]
    return (best, total_a * keep_a + total_b * keep_b, merged)


def gather_pipe(piece, order):
    for name in order:
        piece = lax.all_gather(piece, name, axis=0, tiled=True)
    return piece


def on_device(
    x_first, x_second, stale_kv, w_qkv, w_out, q_gain, k_gain, layout, counts, slot_block
):
    me = lax.axis_index(PIPE)
    n_seq = math.prod(s for _, s in SEQ_PARTS)
    tokens = BPM * BLOCK
    heads = w_qkv.shape[2] // HS
    width = heads * HS
    scale = 1.0 / math.sqrt(HS)
    linked = slot_mask(layout, counts, slot_block)
    total_blocks = linked.shape[0]
    block_ids = jnp.arange(total_blocks, dtype=jnp.int32)
    batch_of = block_ids // BPM
    mine = lax.dynamic_slice_in_dim(linked, me * BPM, BPM, 0)
    own = lax.dynamic_slice_in_dim(mine, me * BPM, BPM, 1)
    remote = mine & (batch_of != me)[None, :]

    stale = gather_pipe(stale_kv[None], PIPE)
    sizes = [s for _, s in PIPE_PARTS]
    remote_stale = remote.reshape(BPM, *sizes).transpose(0, 2, 1).reshape(BPM, -1)

    pair = jnp.stack([x_first, x_second])
    spread = jnp.broadcast_to(pair[:, None], (2, n_seq) + x_first.shape)
    xs = lax.all_to_all(spread, SEQ, 1, 1, tiled=False).reshape(2, tokens, -1)

    def project(x):
        raw = jnp.einsum("rd,cdh->crh", x, w_qkv, preferred_element_type=jnp.float32)
        query = normalize(raw[0], q_gain, HS).astype(jnp.bfloat16)
        keys = normalize(raw[1], k_gain, HS).astype(jnp.bfloat16)
        values = raw[2].astype(jnp.bfloat16)
        return (query, keys, values)

    q1, k1, v1 = project(xs[0])
    q2, k2, v2 = project(xs[1])

    fresh_kv = gather_pipe(jnp.stack([k1, v1])[None], tuple(reversed(PIPE)))
    count = fresh_kv.shape[0] * tokens

    def attend(query, keys, values, piece_k, piece_v, remote):
        query_h = query.reshape(tokens, heads, HS)
        start_part = partial_attend(
            query_h, keys.reshape(tokens, heads, HS), values.reshape(tokens, heads, HS), own, scale
        )
        fresh = partial_attend(
            query_h,
            piece_k.reshape(count, heads, HS),
            piece_v.reshape(count, heads, HS),
            remote,
            scale,
        )
        best, denom_h, numer = merge_parts(start_part, fresh)
        denom = denom_h.T
        attn = (numer / denom[:, :, None]).reshape(tokens, width).astype(jnp.bfloat16)
        part = jnp.dot(attn, w_out, preferred_element_type=jnp.float32).astype(jnp.bfloat16)
        sent = lax.all_to_all(part.reshape(n_seq, tokens // n_seq, -1), SEQ, 0, 0, tiled=False)
        return jnp.sum(sent.astype(jnp.float32), axis=0).astype(jnp.bfloat16)

    out_first = attend(q1, k1, v1, stale[:, 0], stale[:, 1], remote_stale)
    out_first, fresh_kv = lax.optimization_barrier((out_first, fresh_kv))
    out_second = attend(q2, k2, v2, fresh_kv[:, 0], fresh_kv[:, 1], remote)
    return (out_first, out_second)


def solution(mesh):
    names = PIPE_PARTS + SEQ_PARTS
    fine = Mesh(
        np.asarray(mesh.devices).reshape([s for _, s in names]), tuple(n for n, _ in names)
    )
    rows = P(PIPE + SEQ, None)
    placed = (
        rows,
        rows,
        P(None, PIPE, SEQ),
        P(None, None, SEQ),
        P(SEQ, None),
        P(SEQ),
        P(SEQ),
        P(),
        P(),
        P(),
    )
    return jax.shard_map(
        on_device,
        mesh=fine,
        in_specs=placed,
        out_specs=(rows, rows),
        check_vma=False,
    )
```

```python
import math

import jax
import jax.numpy as jnp
import numpy as np
from jax import lax
from jax.sharding import Mesh
from jax.sharding import PartitionSpec as P

HS = 64
BLOCK = 128
BPM = 1


HIGH = lax.Precision.HIGHEST
NEG = -1e30

PIPE_PARTS = (("y", 8), ("zl", 4))
SEQ_PARTS = (("zh", 2), ("x", 4), ("c", 2))
PIPE = tuple(n for n, _ in PIPE_PARTS)
SEQ = tuple(n for n, _ in SEQ_PARTS)


def slot_mask(layout, counts, slot_block):
    total = layout.shape[0]
    width = layout.shape[1]
    blocks = jnp.arange(total, dtype=jnp.int32)
    valid = jnp.arange(width, dtype=jnp.int32)[None, :] < counts[:, None]
    member = jnp.sum(
        ((layout[:, :, None] == blocks[None, None, :]) & valid[:, :, None]).astype(jnp.float32),
        axis=1,
    )
    placed = (slot_block[:, None] == blocks[None, :]).astype(jnp.float32)
    linked = jnp.dot(jnp.dot(placed, member, precision=HIGH), placed.T, precision=HIGH)
    return linked > 0.5


def normalize(raw, gain, size):
    count = raw.shape[0]
    grid = raw.reshape(count, -1, size)
    factor = lax.rsqrt(jnp.mean(grid * grid, axis=2, keepdims=True) + 1e-06)
    return (grid * factor).reshape(count, -1) * gain[None, :]


def partial_attend(query, keys, values, allowed, scale):
    heads = query.shape[1]
    qrows = query.shape[0]
    krows = keys.shape[0]
    scores = jnp.einsum("qhd,khd->hqk", query, keys, preferred_element_type=jnp.float32) * scale
    grid = scores.reshape(heads, qrows // BLOCK, BLOCK, krows // BLOCK, BLOCK)
    keep = allowed[None, :, None, :, None]
    grid = jnp.where(keep, grid, NEG)
    top = jnp.max(grid, axis=(3, 4))
    weights = jnp.where(keep, jnp.exp(grid - top[:, :, :, None, None]), 0.0)
    total = jnp.sum(weights, axis=(3, 4))
    weights = weights.reshape(heads, qrows, krows)
    summed = jnp.einsum("hqk,khd->qhd", weights, values.astype(jnp.float32), precision=HIGH)
    return (top.reshape(heads, qrows), total.reshape(heads, qrows), summed)


def merge_parts(first, second):
    top_a, total_a, summed_a = first
    top_b, total_b, summed_b = second
    best = jnp.maximum(top_a, top_b)
    keep_a = jnp.exp(top_a - best)
    keep_b = jnp.exp(top_b - best)
    merged = summed_a * keep_a.T[:, :, None] + summed_b * keep_b.T[:, :, None]
    return (best, total_a * keep_a + total_b * keep_b, merged)


def gather_pipe(piece, order):
    for name in order:
        piece = lax.all_gather(piece, name, axis=0, tiled=True)
    return piece


def on_device(
    x_first, x_second, stale_kv, w_qkv, w_out, q_gain, k_gain, layout, counts, slot_block
):
    me = lax.axis_index(PIPE)
    n_seq = math.prod(s for _, s in SEQ_PARTS)
    tokens = BPM * BLOCK
    heads = w_qkv.shape[2] // HS
    width = heads * HS
    scale = 1.0 / math.sqrt(HS)
    linked = slot_mask(layout, counts, slot_block)
    total_blocks = linked.shape[0]
    block_ids = jnp.arange(total_blocks, dtype=jnp.int32)
    batch_of = block_ids // BPM
    mine = lax.dynamic_slice_in_dim(linked, me * BPM, BPM, 0)
    own = lax.dynamic_slice_in_dim(mine, me * BPM, BPM, 1)
    remote = mine & (batch_of != me)[None, :]

    stale = gather_pipe(stale_kv[None], PIPE)
    sizes = [s for _, s in PIPE_PARTS]
    remote_stale = remote.reshape(BPM, *sizes).transpose(0, 2, 1).reshape(BPM, -1)

    def exchange_rows(x):
        spread = jnp.broadcast_to(x[None], (n_seq,) + x.shape)
        return lax.all_to_all(spread, SEQ, 0, 0, tiled=False).reshape(tokens, -1)

    def project(x):
        raw = jnp.einsum("rd,cdh->crh", x, w_qkv, preferred_element_type=jnp.float32)
        query = normalize(raw[0], q_gain, HS).astype(jnp.bfloat16)
        keys = normalize(raw[1], k_gain, HS).astype(jnp.bfloat16)
        values = raw[2].astype(jnp.bfloat16)
        return (query, keys, values)

    q1, k1, v1 = project(exchange_rows(x_first))

    fresh_kv = gather_pipe(jnp.stack([k1, v1])[None], tuple(reversed(PIPE)))
    count = fresh_kv.shape[0] * tokens
    q2, k2, v2 = project(exchange_rows(x_second))

    def attend(query, keys, values, piece_k, piece_v, remote):
        query_h = query.reshape(tokens, heads, HS)
        start_part = partial_attend(
            query_h, keys.reshape(tokens, heads, HS), values.reshape(tokens, heads, HS), own, scale
        )
        fresh = partial_attend(
            query_h,
            piece_k.reshape(count, heads, HS),
            piece_v.reshape(count, heads, HS),
            remote,
            scale,
        )
        best, denom_h, numer = merge_parts(start_part, fresh)
        denom = denom_h.T
        attn = (numer / denom[:, :, None]).reshape(tokens, width).astype(jnp.bfloat16)
        part = jnp.dot(attn, w_out, preferred_element_type=jnp.float32).astype(jnp.bfloat16)
        sent = lax.all_to_all(part.reshape(n_seq, tokens // n_seq, -1), SEQ, 0, 0, tiled=False)
        return jnp.sum(sent.astype(jnp.float32), axis=0).astype(jnp.bfloat16)

    out_first = attend(q1, k1, v1, stale[:, 0], stale[:, 1], remote_stale)
    out_first, fresh_kv = lax.optimization_barrier((out_first, fresh_kv))
    out_second = attend(q2, k2, v2, fresh_kv[:, 0], fresh_kv[:, 1], remote)
    return (out_first, out_second)


def solution(mesh):
    names = PIPE_PARTS + SEQ_PARTS
    fine = Mesh(
        np.asarray(mesh.devices).reshape([s for _, s in names]), tuple(n for n, _ in names)
    )
    rows = P(PIPE + SEQ, None)
    placed = (
        rows,
        rows,
        P(None, PIPE, SEQ),
        P(None, None, SEQ),
        P(SEQ, None),
        P(SEQ),
        P(SEQ),
        P(),
        P(),
        P(),
    )
    return jax.shard_map(
        on_device,
        mesh=fine,
        in_specs=placed,
        out_specs=(rows, rows),
        check_vma=False,
    )
```

```python
import math

import jax
import jax.numpy as jnp
import numpy as np
from jax import lax
from jax.sharding import Mesh
from jax.sharding import PartitionSpec as P

HS = 64
BLOCK = 128
BPM = 1


HIGH = lax.Precision.HIGHEST
NEG = -1e30

PIPE_PARTS = (("y", 8), ("zl", 4))
SEQ_PARTS = (("zh", 2), ("x", 4), ("c", 2))
PIPE = tuple(n for n, _ in PIPE_PARTS)
SEQ = tuple(n for n, _ in SEQ_PARTS)


def slot_mask(layout, counts, slot_block):
    total = layout.shape[0]
    width = layout.shape[1]
    blocks = jnp.arange(total, dtype=jnp.int32)
    valid = jnp.arange(width, dtype=jnp.int32)[None, :] < counts[:, None]
    member = jnp.sum(
        ((layout[:, :, None] == blocks[None, None, :]) & valid[:, :, None]).astype(jnp.float32),
        axis=1,
    )
    placed = (slot_block[:, None] == blocks[None, :]).astype(jnp.float32)
    linked = jnp.dot(jnp.dot(placed, member, precision=HIGH), placed.T, precision=HIGH)
    return linked > 0.5


def normalize(raw, gain, size):
    count = raw.shape[0]
    grid = raw.reshape(count, -1, size)
    factor = lax.rsqrt(jnp.mean(grid * grid, axis=2, keepdims=True) + 1e-06)
    return (grid * factor).reshape(count, -1) * gain[None, :]


def partial_attend(query, keys, values, allowed, scale):
    heads = query.shape[1]
    qrows = query.shape[0]
    krows = keys.shape[0]
    scores = jnp.einsum("qhd,khd->hqk", query, keys, preferred_element_type=jnp.float32) * scale
    grid = scores.reshape(heads, qrows // BLOCK, BLOCK, krows // BLOCK, BLOCK)
    keep = allowed[None, :, None, :, None]
    grid = jnp.where(keep, grid, NEG)
    top = jnp.max(grid, axis=(3, 4))
    weights = jnp.where(keep, jnp.exp(grid - top[:, :, :, None, None]), 0.0)
    total = jnp.sum(weights, axis=(3, 4))
    weights = weights.reshape(heads, qrows, krows)
    summed = jnp.einsum("hqk,khd->qhd", weights, values.astype(jnp.float32), precision=HIGH)
    return (top.reshape(heads, qrows), total.reshape(heads, qrows), summed)


def merge_parts(first, second):
    top_a, total_a, summed_a = first
    top_b, total_b, summed_b = second
    best = jnp.maximum(top_a, top_b)
    keep_a = jnp.exp(top_a - best)
    keep_b = jnp.exp(top_b - best)
    merged = summed_a * keep_a.T[:, :, None] + summed_b * keep_b.T[:, :, None]
    return (best, total_a * keep_a + total_b * keep_b, merged)


def gather_pipe(piece, order):
    for name in order:
        piece = lax.all_gather(piece, name, axis=0, tiled=True)
    return piece


def on_device(
    x_first, x_second, stale_kv, w_qkv, w_out, q_gain, k_gain, layout, counts, slot_block
):
    me = lax.axis_index(PIPE)
    n_seq = math.prod(s for _, s in SEQ_PARTS)
    tokens = BPM * BLOCK
    heads = w_qkv.shape[2] // HS
    width = heads * HS
    scale = 1.0 / math.sqrt(HS)
    linked = slot_mask(layout, counts, slot_block)
    total_blocks = linked.shape[0]
    block_ids = jnp.arange(total_blocks, dtype=jnp.int32)
    batch_of = block_ids // BPM
    mine = lax.dynamic_slice_in_dim(linked, me * BPM, BPM, 0)
    own = lax.dynamic_slice_in_dim(mine, me * BPM, BPM, 1)
    remote = mine & (batch_of != me)[None, :]

    near = lax.all_gather(stale_kv[None], PIPE[1], axis=0, tiled=True)
    pair, near = lax.optimization_barrier((jnp.stack([x_first, x_second]), near))
    stale = lax.all_gather(near, PIPE[0], axis=0, tiled=True)

    def exchange_rows(x):
        spread = jnp.broadcast_to(x[:, None], (x.shape[0], n_seq) + x.shape[1:])
        return lax.all_to_all(spread, SEQ, 1, 1, tiled=False).reshape(x.shape[0], tokens, -1)

    def project(x):
        raw = jnp.einsum("rd,cdh->crh", x, w_qkv, preferred_element_type=jnp.float32)
        query = normalize(raw[0], q_gain, HS).astype(jnp.bfloat16)
        keys = normalize(raw[1], k_gain, HS).astype(jnp.bfloat16)
        values = raw[2].astype(jnp.bfloat16)
        return (query, keys, values)

    xs = exchange_rows(pair)
    q1, k1, v1 = project(xs[0])
    q2, k2, v2 = project(xs[1])

    fresh_kv = gather_pipe(jnp.stack([k1, v1])[None], tuple(reversed(PIPE)))
    count = fresh_kv.shape[0] * tokens

    def attend(query, keys, values, piece_k, piece_v, remote):
        query_h = query.reshape(tokens, heads, HS)
        start_part = partial_attend(
            query_h, keys.reshape(tokens, heads, HS), values.reshape(tokens, heads, HS), own, scale
        )
        fresh = partial_attend(
            query_h,
            piece_k.reshape(count, heads, HS),
            piece_v.reshape(count, heads, HS),
            remote,
            scale,
        )
        best, denom_h, numer = merge_parts(start_part, fresh)
        denom = denom_h.T
        attn = (numer / denom[:, :, None]).reshape(tokens, width).astype(jnp.bfloat16)
        part = jnp.dot(attn, w_out, preferred_element_type=jnp.float32).astype(jnp.bfloat16)
        sent = lax.all_to_all(part.reshape(n_seq, tokens // n_seq, -1), SEQ, 0, 0, tiled=False)
        return jnp.sum(sent.astype(jnp.float32), axis=0).astype(jnp.bfloat16)

    out_first = attend(q1, k1, v1, stale[:, 0], stale[:, 1], remote)
    out_first, fresh_kv = lax.optimization_barrier((out_first, fresh_kv))
    out_second = attend(q2, k2, v2, fresh_kv[:, 0], fresh_kv[:, 1], remote)
    return (out_first, out_second)


def solution(mesh):
    names = PIPE_PARTS + SEQ_PARTS
    fine = Mesh(
        np.asarray(mesh.devices).reshape([s for _, s in names]), tuple(n for n, _ in names)
    )
    rows = P(PIPE + SEQ, None)
    placed = (
        rows,
        rows,
        P(None, PIPE, SEQ),
        P(None, None, SEQ),
        P(SEQ, None),
        P(SEQ),
        P(SEQ),
        P(),
        P(),
        P(),
    )
    return jax.shard_map(
        on_device,
        mesh=fine,
        in_specs=placed,
        out_specs=(rows, rows),
        check_vma=False,
    )
```

```python
import functools
import math

import jax
import jax.numpy as jnp
import numpy as np
from jax import lax
from jax.experimental import pallas as pl
from jax.experimental.pallas import tpu as pltpu
from jax.sharding import Mesh
from jax.sharding import PartitionSpec as P

HS = 64
BLOCK = 128
BPM = 1


HIGH = lax.Precision.HIGHEST
NEG = -1e30

PIPE_PARTS = (("y", 8), ("zl", 4))
SEQ_PARTS = (("zh", 2), ("x", 4), ("c", 2))
PIPE = tuple(n for n, _ in PIPE_PARTS)
SEQ = tuple(n for n, _ in SEQ_PARTS)


def slot_mask(layout, counts, slot_block):
    total = layout.shape[0]
    width = layout.shape[1]
    blocks = jnp.arange(total, dtype=jnp.int32)
    valid = jnp.arange(width, dtype=jnp.int32)[None, :] < counts[:, None]
    member = jnp.sum(
        ((layout[:, :, None] == blocks[None, None, :]) & valid[:, :, None]).astype(jnp.float32),
        axis=1,
    )
    placed = (slot_block[:, None] == blocks[None, :]).astype(jnp.float32)
    linked = jnp.dot(jnp.dot(placed, member, precision=HIGH), placed.T, precision=HIGH)
    return linked > 0.5


def normalize(raw, gain, size):
    count = raw.shape[0]
    grid = raw.reshape(count, -1, size)
    factor = lax.rsqrt(jnp.mean(grid * grid, axis=2, keepdims=True) + 1e-06)
    return (grid * factor).reshape(count, -1) * gain[None, :]


def attn_kernel(allowed_ref, q_ref, k_ref, v_ref, kv_ref, o_ref, *, scale, n_blocks):
    q = q_ref[...]
    rows, width = q.shape
    lane = lax.broadcasted_iota(jnp.int32, (rows, width), 1)
    first = lane < HS
    zero = jnp.zeros_like(q)
    q0 = jnp.where(first, q, zero)
    q1 = jnp.where(first, zero, q)

    def scores(kb):
        dims = (((1,), (1,)), ((), ()))
        s0 = lax.dot_general(q0, kb, dims, preferred_element_type=jnp.float32) * scale
        s1 = lax.dot_general(q1, kb, dims, preferred_element_type=jnp.float32) * scale
        return s0, s1

    def update(carry, s0, s1, vb):
        m0, m1, l0, l1, acc = carry
        n0 = jnp.maximum(m0, jnp.max(s0, axis=1, keepdims=True))
        n1 = jnp.maximum(m1, jnp.max(s1, axis=1, keepdims=True))
        a0 = jnp.exp(m0 - n0)
        a1 = jnp.exp(m1 - n1)
        p0 = jnp.exp(s0 - n0)
        p1 = jnp.exp(s1 - n1)
        l0 = l0 * a0 + jnp.sum(p0, axis=1, keepdims=True)
        l1 = l1 * a1 + jnp.sum(p1, axis=1, keepdims=True)
        pv0 = jnp.dot(p0.astype(vb.dtype), vb, preferred_element_type=jnp.float32)
        pv1 = jnp.dot(p1.astype(vb.dtype), vb, preferred_element_type=jnp.float32)
        acc = acc * jnp.where(first, a0, a1) + jnp.where(first, pv0, pv1)
        return (n0, n1, l0, l1, acc)

    init = (
        jnp.full((rows, 1), NEG, jnp.float32),
        jnp.full((rows, 1), NEG, jnp.float32),
        jnp.zeros((rows, 1), jnp.float32),
        jnp.zeros((rows, 1), jnp.float32),
        jnp.zeros((rows, width), jnp.float32),
    )
    s0, s1 = scores(k_ref[...])
    carry = update(init, s0, s1, v_ref[...])

    def body(b, carry):
        keep = allowed_ref[b] > 0
        s0, s1 = scores(kv_ref[b, 0])
        s0 = jnp.where(keep, s0, NEG)
        s1 = jnp.where(keep, s1, NEG)
        return update(carry, s0, s1, kv_ref[b, 1])

    m0, m1, l0, l1, acc = lax.fori_loop(0, n_blocks, body, carry)
    o_ref[...] = (acc / jnp.where(first, l0, l1)).astype(o_ref.dtype)


def block_attend(allowed, query, keys, values, kv, scale):
    n_blocks = kv.shape[0]
    vmem = pltpu.MemorySpace.VMEM
    return pl.pallas_call(
        functools.partial(attn_kernel, scale=scale, n_blocks=n_blocks),
        out_shape=jax.ShapeDtypeStruct(query.shape, jnp.bfloat16),
        in_specs=[pl.BlockSpec(memory_space=pltpu.MemorySpace.SMEM)] + [pl.BlockSpec(memory_space=vmem)] * 4,
        out_specs=pl.BlockSpec(memory_space=vmem),
    )(allowed, query, keys, values, kv)


def gather_pipe(piece, order):
    for name in order:
        piece = lax.all_gather(piece, name, axis=0, tiled=True)
    return piece


def on_device(
    x_first, x_second, stale_kv, w_qkv, w_out, q_gain, k_gain, layout, counts, slot_block
):
    me = lax.axis_index(PIPE)
    n_seq = math.prod(s for _, s in SEQ_PARTS)
    tokens = BPM * BLOCK
    heads = w_qkv.shape[2] // HS
    width = heads * HS
    scale = 1.0 / math.sqrt(HS)
    linked = slot_mask(layout, counts, slot_block)
    total_blocks = linked.shape[0]
    block_ids = jnp.arange(total_blocks, dtype=jnp.int32)
    batch_of = block_ids // BPM
    mine = lax.dynamic_slice_in_dim(linked, me * BPM, BPM, 0)
    remote = mine & (batch_of != me)[None, :]

    near = lax.all_gather(stale_kv[None], PIPE[1], axis=0, tiled=True)
    pair, near = lax.optimization_barrier((jnp.stack([x_first, x_second]), near))
    stale = lax.all_gather(near, PIPE[0], axis=0, tiled=True)

    def exchange_rows(x):
        spread = jnp.broadcast_to(x[:, None], (x.shape[0], n_seq) + x.shape[1:])
        return lax.all_to_all(spread, SEQ, 1, 1, tiled=False).reshape(x.shape[0], tokens, -1)

    def project(x):
        raw = jnp.einsum("rd,cdh->crh", x, w_qkv, preferred_element_type=jnp.float32)
        query = normalize(raw[0], q_gain, HS).astype(jnp.bfloat16)
        keys = normalize(raw[1], k_gain, HS).astype(jnp.bfloat16)
        values = raw[2].astype(jnp.bfloat16)
        return (query, keys, values)

    xs = exchange_rows(pair)
    q1, k1, v1 = project(xs[0])
    q2, k2, v2 = project(xs[1])

    fresh_kv = gather_pipe(jnp.stack([k1, v1])[None], tuple(reversed(PIPE)))

    def attend(query, keys, values, kv, remote):
        allowed = remote[0].astype(jnp.int32)
        attn = block_attend(allowed, query, keys, values, kv, scale)
        part = jnp.dot(attn, w_out, preferred_element_type=jnp.float32).astype(jnp.bfloat16)
        sent = lax.all_to_all(part.reshape(n_seq, tokens // n_seq, -1), SEQ, 0, 0, tiled=False)
        return jnp.sum(sent.astype(jnp.float32), axis=0).astype(jnp.bfloat16)

    out_first = attend(q1, k1, v1, stale, remote)
    out_first, fresh_kv = lax.optimization_barrier((out_first, fresh_kv))
    out_second = attend(q2, k2, v2, fresh_kv, remote)
    return (out_first, out_second)


def solution(mesh):
    names = PIPE_PARTS + SEQ_PARTS
    fine = Mesh(
        np.asarray(mesh.devices).reshape([s for _, s in names]), tuple(n for n, _ in names)
    )
    rows = P(PIPE + SEQ, None)
    placed = (
        rows,
        rows,
        P(None, PIPE, SEQ),
        P(None, None, SEQ),
        P(SEQ, None),
        P(SEQ),
        P(SEQ),
        P(),
        P(),
        P(),
    )
    return jax.shard_map(
        on_device,
        mesh=fine,
        in_specs=placed,
        out_specs=(rows, rows),
        check_vma=False,
    )
```

```python
import functools
import math

import jax
import jax.numpy as jnp
import numpy as np
from jax import lax
from jax.experimental import pallas as pl
from jax.experimental.pallas import tpu as pltpu
from jax.sharding import Mesh
from jax.sharding import PartitionSpec as P

HS = 64
BLOCK = 128
BPM = 1


HIGH = lax.Precision.HIGHEST
NEG = -1e30

PIPE_PARTS = (("y", 8), ("zl", 4))
SEQ_PARTS = (("zh", 2), ("x", 4), ("c", 2))
PIPE = tuple(n for n, _ in PIPE_PARTS)
SEQ = tuple(n for n, _ in SEQ_PARTS)


def slot_mask(layout, counts, slot_block):
    total = layout.shape[0]
    width = layout.shape[1]
    blocks = jnp.arange(total, dtype=jnp.int32)
    valid = jnp.arange(width, dtype=jnp.int32)[None, :] < counts[:, None]
    member = jnp.sum(
        ((layout[:, :, None] == blocks[None, None, :]) & valid[:, :, None]).astype(jnp.float32),
        axis=1,
    )
    placed = (slot_block[:, None] == blocks[None, :]).astype(jnp.float32)
    linked = jnp.dot(jnp.dot(placed, member, precision=HIGH), placed.T, precision=HIGH)
    return linked > 0.5


def normalize(raw, gain, size):
    count = raw.shape[0]
    grid = raw.reshape(count, -1, size)
    factor = lax.rsqrt(jnp.mean(grid * grid, axis=2, keepdims=True) + 1e-06)
    return (grid * factor).reshape(count, -1) * gain[None, :]


def attn_kernel(allowed_ref, q_ref, k_ref, v_ref, kv_ref, o_ref, *, scale, n_blocks):
    q = q_ref[...] * jnp.asarray(scale, q_ref.dtype)
    rows, width = q.shape
    lane = lax.broadcasted_iota(jnp.int32, (rows, width), 1)
    first = lane < HS
    zero = jnp.zeros_like(q)
    q0 = jnp.where(first, q, zero)
    q1 = jnp.where(first, zero, q)

    def scores(kb):
        dims = (((1,), (1,)), ((), ()))
        s0 = lax.dot_general(q0, kb, dims, preferred_element_type=jnp.float32)
        s1 = lax.dot_general(q1, kb, dims, preferred_element_type=jnp.float32)
        return s0, s1

    def update(carry, s0, s1, vb):
        m0, m1, l0, l1, acc = carry
        n0 = jnp.maximum(m0, jnp.max(s0, axis=1, keepdims=True))
        n1 = jnp.maximum(m1, jnp.max(s1, axis=1, keepdims=True))
        a0 = jnp.exp(m0 - n0)
        a1 = jnp.exp(m1 - n1)
        p0 = jnp.exp(s0 - n0)
        p1 = jnp.exp(s1 - n1)
        l0 = l0 * a0 + jnp.sum(p0, axis=1, keepdims=True)
        l1 = l1 * a1 + jnp.sum(p1, axis=1, keepdims=True)
        pv0 = jnp.dot(p0.astype(vb.dtype), vb, preferred_element_type=jnp.float32)
        pv1 = jnp.dot(p1.astype(vb.dtype), vb, preferred_element_type=jnp.float32)
        acc = acc * jnp.where(first, a0, a1) + jnp.where(first, pv0, pv1)
        return (n0, n1, l0, l1, acc)

    init = (
        jnp.full((rows, 1), NEG, jnp.float32),
        jnp.full((rows, 1), NEG, jnp.float32),
        jnp.zeros((rows, 1), jnp.float32),
        jnp.zeros((rows, 1), jnp.float32),
        jnp.zeros((rows, width), jnp.float32),
    )
    s0, s1 = scores(k_ref[...])
    carry = update(init, s0, s1, v_ref[...])

    def visit(b, carry):
        s0, s1 = scores(kv_ref[b, 0])
        return update(carry, s0, s1, kv_ref[b, 1])

    def body(b, carry):
        return lax.cond(allowed_ref[b] > 0, functools.partial(visit, b), lambda c: c, carry)

    m0, m1, l0, l1, acc = lax.fori_loop(0, n_blocks, body, carry)
    o_ref[...] = (acc / jnp.where(first, l0, l1)).astype(o_ref.dtype)


def block_attend(allowed, query, keys, values, kv, scale):
    n_blocks = kv.shape[0]
    vmem = pltpu.MemorySpace.VMEM
    return pl.pallas_call(
        functools.partial(attn_kernel, scale=scale, n_blocks=n_blocks),
        out_shape=jax.ShapeDtypeStruct(query.shape, jnp.bfloat16),
        in_specs=[pl.BlockSpec(memory_space=pltpu.MemorySpace.SMEM)] + [pl.BlockSpec(memory_space=vmem)] * 4,
        out_specs=pl.BlockSpec(memory_space=vmem),
    )(allowed, query, keys, values, kv)


def gather_pipe(piece, order):
    for name in order:
        piece = lax.all_gather(piece, name, axis=0, tiled=True)
    return piece


def on_device(
    x_first, x_second, stale_kv, w_qkv, w_out, q_gain, k_gain, layout, counts, slot_block
):
    me = lax.axis_index(PIPE)
    n_seq = math.prod(s for _, s in SEQ_PARTS)
    tokens = BPM * BLOCK
    heads = w_qkv.shape[2] // HS
    width = heads * HS
    scale = 1.0 / math.sqrt(HS)
    linked = slot_mask(layout, counts, slot_block)
    total_blocks = linked.shape[0]
    block_ids = jnp.arange(total_blocks, dtype=jnp.int32)
    batch_of = block_ids // BPM
    mine = lax.dynamic_slice_in_dim(linked, me * BPM, BPM, 0)
    remote = mine & (batch_of != me)[None, :]

    near = lax.all_gather(stale_kv[None], PIPE[1], axis=0, tiled=True)
    pair, near = lax.optimization_barrier((jnp.stack([x_first, x_second]), near))
    stale = lax.all_gather(near, PIPE[0], axis=0, tiled=True)

    def exchange_rows(x):
        spread = jnp.broadcast_to(x[:, None], (x.shape[0], n_seq) + x.shape[1:])
        return lax.all_to_all(spread, SEQ, 1, 1, tiled=False).reshape(x.shape[0], tokens, -1)

    def project(x):
        raw = jnp.einsum("rd,cdh->crh", x, w_qkv, preferred_element_type=jnp.float32)
        query = normalize(raw[0], q_gain, HS).astype(jnp.bfloat16)
        keys = normalize(raw[1], k_gain, HS).astype(jnp.bfloat16)
        values = raw[2].astype(jnp.bfloat16)
        return (query, keys, values)

    xs = exchange_rows(pair)
    q1, k1, v1 = project(xs[0])
    q2, k2, v2 = project(xs[1])

    fresh_kv = gather_pipe(jnp.stack([k1, v1])[None], tuple(reversed(PIPE)))

    def attend(query, keys, values, kv, remote):
        allowed = remote[0].astype(jnp.int32)
        attn = block_attend(allowed, query, keys, values, kv, scale)
        part = jnp.dot(attn, w_out, preferred_element_type=jnp.float32).astype(jnp.bfloat16)
        sent = lax.all_to_all(part.reshape(n_seq, tokens // n_seq, -1), SEQ, 0, 0, tiled=False)
        return jnp.sum(sent.astype(jnp.float32), axis=0).astype(jnp.bfloat16)

    out_first = attend(q1, k1, v1, stale, remote)
    out_first, fresh_kv = lax.optimization_barrier((out_first, fresh_kv))
    out_second = attend(q2, k2, v2, fresh_kv, remote)
    return (out_first, out_second)


def solution(mesh):
    names = PIPE_PARTS + SEQ_PARTS
    fine = Mesh(
        np.asarray(mesh.devices).reshape([s for _, s in names]), tuple(n for n, _ in names)
    )
    rows = P(PIPE + SEQ, None)
    placed = (
        rows,
        rows,
        P(None, PIPE, SEQ),
        P(None, None, SEQ),
        P(SEQ, None),
        P(SEQ),
        P(SEQ),
        P(),
        P(),
        P(),
    )
    return jax.shard_map(
        on_device,
        mesh=fine,
        in_specs=placed,
        out_specs=(rows, rows),
        check_vma=False,
    )
```

```python
import functools
import math

import jax
import jax.numpy as jnp
import numpy as np
from jax import lax
from jax.experimental import pallas as pl
from jax.experimental.pallas import tpu as pltpu
from jax.sharding import Mesh
from jax.sharding import PartitionSpec as P

HS = 64
BLOCK = 128
BPM = 1


HIGH = lax.Precision.HIGHEST
NEG = -1e30

PIPE_PARTS = (("y", 8), ("zl", 4))
SEQ_PARTS = (("zh", 2), ("x", 4), ("c", 2))
PIPE = tuple(n for n, _ in PIPE_PARTS)
SEQ = tuple(n for n, _ in SEQ_PARTS)


def slot_mask(layout, counts, slot_block):
    total = layout.shape[0]
    width = layout.shape[1]
    blocks = jnp.arange(total, dtype=jnp.int32)
    valid = jnp.arange(width, dtype=jnp.int32)[None, :] < counts[:, None]
    member = jnp.sum(
        ((layout[:, :, None] == blocks[None, None, :]) & valid[:, :, None]).astype(jnp.float32),
        axis=1,
    )
    placed = (slot_block[:, None] == blocks[None, :]).astype(jnp.float32)
    linked = jnp.dot(jnp.dot(placed, member, precision=HIGH), placed.T, precision=HIGH)
    return linked > 0.5


def normalize(raw, gain, size):
    count = raw.shape[0]
    grid = raw.reshape(count, -1, size)
    factor = lax.rsqrt(jnp.mean(grid * grid, axis=2, keepdims=True) + 1e-06)
    return (grid * factor).reshape(count, -1) * gain[None, :]


def attn_kernel(allowed_ref, q_ref, k_ref, v_ref, kv_ref, o_ref, *, scale, n_blocks):
    q = q_ref[...] * jnp.asarray(scale, q_ref.dtype)
    rows, width = q.shape
    lane = lax.broadcasted_iota(jnp.int32, (rows, width), 1)
    zero = jnp.zeros_like(q)
    qt0 = jnp.where(lane < HS, q, zero).T
    qt1 = jnp.where(lane < HS, zero, q).T
    first = lax.broadcasted_iota(jnp.int32, (width, rows), 0) < HS

    def update(carry, kb, vb):
        m0, m1, l0, l1, acc = carry
        s0 = jnp.dot(kb, qt0, preferred_element_type=jnp.float32)
        s1 = jnp.dot(kb, qt1, preferred_element_type=jnp.float32)
        n0 = jnp.maximum(m0, jnp.max(s0, axis=0, keepdims=True))
        n1 = jnp.maximum(m1, jnp.max(s1, axis=0, keepdims=True))
        a0 = jnp.exp(m0 - n0)
        a1 = jnp.exp(m1 - n1)
        p0 = jnp.exp(s0 - n0)
        p1 = jnp.exp(s1 - n1)
        l0 = l0 * a0 + jnp.sum(p0, axis=0, keepdims=True)
        l1 = l1 * a1 + jnp.sum(p1, axis=0, keepdims=True)
        vt = vb.T
        pv0 = jnp.dot(vt, p0.astype(vb.dtype), preferred_element_type=jnp.float32)
        pv1 = jnp.dot(vt, p1.astype(vb.dtype), preferred_element_type=jnp.float32)
        acc = acc * jnp.where(first, a0, a1) + jnp.where(first, pv0, pv1)
        return (n0, n1, l0, l1, acc)

    init = (
        jnp.full((1, rows), NEG, jnp.float32),
        jnp.full((1, rows), NEG, jnp.float32),
        jnp.zeros((1, rows), jnp.float32),
        jnp.zeros((1, rows), jnp.float32),
        jnp.zeros((width, rows), jnp.float32),
    )
    carry = update(init, k_ref[...], v_ref[...])

    def visit(b, carry):
        return update(carry, kv_ref[b, 0], kv_ref[b, 1])

    def body(b, carry):
        return lax.cond(allowed_ref[b] > 0, functools.partial(visit, b), lambda c: c, carry)

    m0, m1, l0, l1, acc = lax.fori_loop(0, n_blocks, body, carry)
    o_ref[...] = (acc / jnp.where(first, l0, l1)).T.astype(o_ref.dtype)


def block_attend(allowed, query, keys, values, kv, scale):
    n_blocks = kv.shape[0]
    vmem = pltpu.MemorySpace.VMEM
    return pl.pallas_call(
        functools.partial(attn_kernel, scale=scale, n_blocks=n_blocks),
        out_shape=jax.ShapeDtypeStruct(query.shape, jnp.bfloat16),
        in_specs=[pl.BlockSpec(memory_space=pltpu.MemorySpace.SMEM)] + [pl.BlockSpec(memory_space=vmem)] * 4,
        out_specs=pl.BlockSpec(memory_space=vmem),
    )(allowed, query, keys, values, kv)


def gather_pipe(piece, order):
    for name in order:
        piece = lax.all_gather(piece, name, axis=0, tiled=True)
    return piece


def on_device(
    x_first, x_second, stale_kv, w_qkv, w_out, q_gain, k_gain, layout, counts, slot_block
):
    me = lax.axis_index(PIPE)
    n_seq = math.prod(s for _, s in SEQ_PARTS)
    tokens = BPM * BLOCK
    heads = w_qkv.shape[2] // HS
    width = heads * HS
    scale = 1.0 / math.sqrt(HS)
    linked = slot_mask(layout, counts, slot_block)
    total_blocks = linked.shape[0]
    block_ids = jnp.arange(total_blocks, dtype=jnp.int32)
    batch_of = block_ids // BPM
    mine = lax.dynamic_slice_in_dim(linked, me * BPM, BPM, 0)
    remote = mine & (batch_of != me)[None, :]

    near = lax.all_gather(stale_kv[None], PIPE[1], axis=0, tiled=True)
    pair, near = lax.optimization_barrier((jnp.stack([x_first, x_second]), near))
    stale = lax.all_gather(near, PIPE[0], axis=0, tiled=True)

    def exchange_rows(x):
        spread = jnp.broadcast_to(x[:, None], (x.shape[0], n_seq) + x.shape[1:])
        return lax.all_to_all(spread, SEQ, 1, 1, tiled=False).reshape(x.shape[0], tokens, -1)

    def project(x):
        raw = jnp.einsum("rd,cdh->crh", x, w_qkv, preferred_element_type=jnp.float32)
        query = normalize(raw[0], q_gain, HS).astype(jnp.bfloat16)
        keys = normalize(raw[1], k_gain, HS).astype(jnp.bfloat16)
        values = raw[2].astype(jnp.bfloat16)
        return (query, keys, values)

    xs = exchange_rows(pair)
    q1, k1, v1 = project(xs[0])
    q2, k2, v2 = project(xs[1])

    fresh_kv = gather_pipe(jnp.stack([k1, v1])[None], tuple(reversed(PIPE)))

    def attend(query, keys, values, kv, remote):
        allowed = remote[0].astype(jnp.int32)
        attn = block_attend(allowed, query, keys, values, kv, scale)
        part = jnp.dot(attn, w_out, preferred_element_type=jnp.float32).astype(jnp.bfloat16)
        sent = lax.all_to_all(part.reshape(n_seq, tokens // n_seq, -1), SEQ, 0, 0, tiled=False)
        return jnp.sum(sent.astype(jnp.float32), axis=0).astype(jnp.bfloat16)

    out_first = attend(q1, k1, v1, stale, remote)
    out_first, fresh_kv = lax.optimization_barrier((out_first, fresh_kv))
    out_second = attend(q2, k2, v2, fresh_kv, remote)
    return (out_first, out_second)


def solution(mesh):
    names = PIPE_PARTS + SEQ_PARTS
    fine = Mesh(
        np.asarray(mesh.devices).reshape([s for _, s in names]), tuple(n for n, _ in names)
    )
    rows = P(PIPE + SEQ, None)
    placed = (
        rows,
        rows,
        P(None, PIPE, SEQ),
        P(None, None, SEQ),
        P(SEQ, None),
        P(SEQ),
        P(SEQ),
        P(),
        P(),
        P(),
    )
    return jax.shard_map(
        on_device,
        mesh=fine,
        in_specs=placed,
        out_specs=(rows, rows),
        check_vma=False,
    )
```

```python
import functools
import math

import jax
import jax.numpy as jnp
import numpy as np
from jax import lax
from jax.experimental import pallas as pl
from jax.experimental.pallas import tpu as pltpu
from jax.sharding import Mesh
from jax.sharding import PartitionSpec as P

HS = 64
BLOCK = 128
BPM = 1


HIGH = lax.Precision.HIGHEST
NEG = -1e30

PIPE_PARTS = (("y", 8), ("zl", 4))
SEQ_PARTS = (("zh", 2), ("x", 4), ("c", 2))
PIPE = tuple(n for n, _ in PIPE_PARTS)
SEQ = tuple(n for n, _ in SEQ_PARTS)


def slot_mask(layout, counts, slot_block):
    total = layout.shape[0]
    width = layout.shape[1]
    blocks = jnp.arange(total, dtype=jnp.int32)
    valid = jnp.arange(width, dtype=jnp.int32)[None, :] < counts[:, None]
    member = jnp.sum(
        ((layout[:, :, None] == blocks[None, None, :]) & valid[:, :, None]).astype(jnp.float32),
        axis=1,
    )
    placed = (slot_block[:, None] == blocks[None, :]).astype(jnp.float32)
    linked = jnp.dot(jnp.dot(placed, member, precision=HIGH), placed.T, precision=HIGH)
    return linked > 0.5


def normalize(raw, gain, size):
    count = raw.shape[0]
    grid = raw.reshape(count, -1, size)
    factor = lax.rsqrt(jnp.mean(grid * grid, axis=2, keepdims=True) + 1e-06)
    return (grid * factor).reshape(count, -1) * gain[None, :]


def attn_kernel(allowed_ref, q_ref, k_ref, v_ref, kv_ref, o_ref, *, scale, n_blocks):
    q = q_ref[...] * jnp.asarray(scale, q_ref.dtype)
    rows, width = q.shape
    lane = lax.broadcasted_iota(jnp.int32, (rows, width), 1)
    zero = jnp.zeros_like(q)
    qt0 = jnp.where(lane < HS, q, zero).T
    qt1 = jnp.where(lane < HS, zero, q).T
    first = lax.broadcasted_iota(jnp.int32, (width, rows), 0) < HS

    def update(carry, kb, vb):
        m0, m1, l0, l1, acc = carry
        s0 = jnp.dot(kb, qt0, preferred_element_type=jnp.float32)
        s1 = jnp.dot(kb, qt1, preferred_element_type=jnp.float32)
        n0 = jnp.maximum(m0, jnp.max(s0, axis=0, keepdims=True))
        n1 = jnp.maximum(m1, jnp.max(s1, axis=0, keepdims=True))
        a0 = jnp.exp(m0 - n0)
        a1 = jnp.exp(m1 - n1)
        p0 = jnp.exp(s0 - n0)
        p1 = jnp.exp(s1 - n1)
        l0 = l0 * a0 + jnp.sum(p0, axis=0, keepdims=True)
        l1 = l1 * a1 + jnp.sum(p1, axis=0, keepdims=True)
        vt = vb.T
        pv0 = jnp.dot(vt, p0.astype(vb.dtype), preferred_element_type=jnp.float32)
        pv1 = jnp.dot(vt, p1.astype(vb.dtype), preferred_element_type=jnp.float32)
        acc = acc * jnp.where(first, a0, a1) + jnp.where(first, pv0, pv1)
        return (n0, n1, l0, l1, acc)

    init = (
        jnp.full((1, rows), NEG, jnp.float32),
        jnp.full((1, rows), NEG, jnp.float32),
        jnp.zeros((1, rows), jnp.float32),
        jnp.zeros((1, rows), jnp.float32),
        jnp.zeros((width, rows), jnp.float32),
    )
    carry = update(init, k_ref[...], v_ref[...])

    def visit(b, carry):
        return update(carry, kv_ref[b, 0], kv_ref[b, 1])

    def body(b, carry):
        return lax.cond(allowed_ref[b] > 0, functools.partial(visit, b), lambda c: c, carry)

    m0, m1, l0, l1, acc = lax.fori_loop(0, n_blocks, body, carry)
    o_ref[...] = (acc / jnp.where(first, l0, l1)).T.astype(o_ref.dtype)


def block_attend(allowed, query, keys, values, kv, scale):
    n_blocks = kv.shape[0]
    vmem = pltpu.MemorySpace.VMEM
    return pl.pallas_call(
        functools.partial(attn_kernel, scale=scale, n_blocks=n_blocks),
        out_shape=jax.ShapeDtypeStruct(query.shape, jnp.bfloat16),
        in_specs=[pl.BlockSpec(memory_space=pltpu.MemorySpace.SMEM)] + [pl.BlockSpec(memory_space=vmem)] * 4,
        out_specs=pl.BlockSpec(memory_space=vmem),
    )(allowed, query, keys, values, kv)


def on_device(
    x_first, x_second, stale_kv, w_qkv, w_out, q_gain, k_gain, layout, counts, slot_block
):
    me = lax.axis_index(PIPE)
    n_seq = math.prod(s for _, s in SEQ_PARTS)
    tokens = BPM * BLOCK
    heads = w_qkv.shape[2] // HS
    width = heads * HS
    scale = 1.0 / math.sqrt(HS)
    linked = slot_mask(layout, counts, slot_block)
    total_blocks = linked.shape[0]
    block_ids = jnp.arange(total_blocks, dtype=jnp.int32)
    batch_of = block_ids // BPM
    mine = lax.dynamic_slice_in_dim(linked, me * BPM, BPM, 0)
    remote = mine & (batch_of != me)[None, :]

    near = lax.all_gather(stale_kv[None], PIPE[1], axis=0, tiled=True)
    first_rows, near = lax.optimization_barrier((x_first, near))
    stale = lax.all_gather(near, PIPE[0], axis=0, tiled=True)

    def exchange_rows(x):
        spread = jnp.broadcast_to(x[:, None], (x.shape[0], n_seq) + x.shape[1:])
        return lax.all_to_all(spread, SEQ, 1, 1, tiled=False).reshape(x.shape[0], tokens, -1)

    def project(x):
        raw = jnp.einsum("rd,cdh->crh", x, w_qkv, preferred_element_type=jnp.float32)
        query = normalize(raw[0], q_gain, HS).astype(jnp.bfloat16)
        keys = normalize(raw[1], k_gain, HS).astype(jnp.bfloat16)
        values = raw[2].astype(jnp.bfloat16)
        return (query, keys, values)

    q1, k1, v1 = project(exchange_rows(first_rows[None])[0])

    near_fresh = lax.all_gather(jnp.stack([k1, v1])[None], PIPE[1], axis=0, tiled=True)
    second_rows, near_fresh = lax.optimization_barrier((x_second, near_fresh))
    fresh_kv = lax.all_gather(near_fresh, PIPE[0], axis=0, tiled=True)
    q2, k2, v2 = project(exchange_rows(second_rows[None])[0])

    def attend(query, keys, values, kv, remote):
        allowed = remote[0].astype(jnp.int32)
        attn = block_attend(allowed, query, keys, values, kv, scale)
        part = jnp.dot(attn, w_out, preferred_element_type=jnp.float32).astype(jnp.bfloat16)
        sent = lax.all_to_all(part.reshape(n_seq, tokens // n_seq, -1), SEQ, 0, 0, tiled=False)
        return jnp.sum(sent.astype(jnp.float32), axis=0).astype(jnp.bfloat16)

    out_first = attend(q1, k1, v1, stale, remote)
    out_first, fresh_kv = lax.optimization_barrier((out_first, fresh_kv))
    out_second = attend(q2, k2, v2, fresh_kv, remote)
    return (out_first, out_second)


def solution(mesh):
    names = PIPE_PARTS + SEQ_PARTS
    fine = Mesh(
        np.asarray(mesh.devices).reshape([s for _, s in names]), tuple(n for n, _ in names)
    )
    rows = P(PIPE + SEQ, None)
    placed = (
        rows,
        rows,
        P(None, PIPE, SEQ),
        P(None, None, SEQ),
        P(SEQ, None),
        P(SEQ),
        P(SEQ),
        P(),
        P(),
        P(),
    )
    return jax.shard_map(
        on_device,
        mesh=fine,
        in_specs=placed,
        out_specs=(rows, rows),
        check_vma=False,
    )
```

```python
import functools
import math

import jax
import jax.numpy as jnp
import numpy as np
from jax import lax
from jax.experimental import pallas as pl
from jax.experimental.pallas import tpu as pltpu
from jax.sharding import Mesh
from jax.sharding import PartitionSpec as P

HS = 64
BLOCK = 128
BPM = 1


HIGH = lax.Precision.HIGHEST
NEG = -1e30

PIPE_PARTS = (("y", 8), ("zl", 4))
SEQ_PARTS = (("zh", 2), ("x", 4), ("c", 2))
PIPE = tuple(n for n, _ in PIPE_PARTS)
SEQ = tuple(n for n, _ in SEQ_PARTS)


def slot_mask(layout, counts, slot_block):
    total = layout.shape[0]
    width = layout.shape[1]
    blocks = jnp.arange(total, dtype=jnp.int32)
    valid = jnp.arange(width, dtype=jnp.int32)[None, :] < counts[:, None]
    member = jnp.sum(
        ((layout[:, :, None] == blocks[None, None, :]) & valid[:, :, None]).astype(jnp.float32),
        axis=1,
    )
    placed = (slot_block[:, None] == blocks[None, :]).astype(jnp.float32)
    linked = jnp.dot(jnp.dot(placed, member, precision=HIGH), placed.T, precision=HIGH)
    return linked > 0.5


def normalize(raw, gain, size):
    count = raw.shape[0]
    grid = raw.reshape(count, -1, size)
    factor = lax.rsqrt(jnp.mean(grid * grid, axis=2, keepdims=True) + 1e-06)
    return (grid * factor).reshape(count, -1) * gain[None, :]


def attn_kernel(allowed_ref, q_ref, k_ref, v_ref, kv_ref, o_ref, *, scale, n_blocks):
    q = q_ref[...] * jnp.asarray(scale, q_ref.dtype)
    rows, width = q.shape
    lane = lax.broadcasted_iota(jnp.int32, (rows, width), 1)
    zero = jnp.zeros_like(q)
    qt0 = jnp.where(lane < HS, q, zero).T
    qt1 = jnp.where(lane < HS, zero, q).T
    first = lax.broadcasted_iota(jnp.int32, (width, rows), 0) < HS

    def update(carry, kb, vb):
        m0, m1, l0, l1, acc = carry
        s0 = jnp.dot(kb, qt0, preferred_element_type=jnp.float32)
        s1 = jnp.dot(kb, qt1, preferred_element_type=jnp.float32)
        n0 = jnp.maximum(m0, jnp.max(s0, axis=0, keepdims=True))
        n1 = jnp.maximum(m1, jnp.max(s1, axis=0, keepdims=True))
        a0 = jnp.exp(m0 - n0)
        a1 = jnp.exp(m1 - n1)
        p0 = jnp.exp(s0 - n0)
        p1 = jnp.exp(s1 - n1)
        l0 = l0 * a0 + jnp.sum(p0, axis=0, keepdims=True)
        l1 = l1 * a1 + jnp.sum(p1, axis=0, keepdims=True)
        vt = vb.T
        pv0 = jnp.dot(vt, p0.astype(vb.dtype), preferred_element_type=jnp.float32)
        pv1 = jnp.dot(vt, p1.astype(vb.dtype), preferred_element_type=jnp.float32)
        acc = acc * jnp.where(first, a0, a1) + jnp.where(first, pv0, pv1)
        return (n0, n1, l0, l1, acc)

    init = (
        jnp.full((1, rows), NEG, jnp.float32),
        jnp.full((1, rows), NEG, jnp.float32),
        jnp.zeros((1, rows), jnp.float32),
        jnp.zeros((1, rows), jnp.float32),
        jnp.zeros((width, rows), jnp.float32),
    )
    carry = update(init, k_ref[...], v_ref[...])

    def visit(b, carry):
        return update(carry, kv_ref[b, 0], kv_ref[b, 1])

    def body(b, carry):
        return lax.cond(allowed_ref[b] > 0, functools.partial(visit, b), lambda c: c, carry)

    m0, m1, l0, l1, acc = lax.fori_loop(0, n_blocks, body, carry)
    o_ref[...] = (acc / jnp.where(first, l0, l1)).T.astype(o_ref.dtype)


def block_attend(allowed, query, keys, values, kv, scale):
    n_blocks = kv.shape[0]
    vmem = pltpu.MemorySpace.VMEM
    return pl.pallas_call(
        functools.partial(attn_kernel, scale=scale, n_blocks=n_blocks),
        out_shape=jax.ShapeDtypeStruct(query.shape, jnp.bfloat16),
        in_specs=[pl.BlockSpec(memory_space=pltpu.MemorySpace.SMEM)] + [pl.BlockSpec(memory_space=vmem)] * 4,
        out_specs=pl.BlockSpec(memory_space=vmem),
    )(allowed, query, keys, values, kv)


def ring_gather(piece, name, size):
    left = [(i, (i + 1) % size) for i in range(size)]
    right = [(i, (i - 1) % size) for i in range(size)]
    got = {0: piece}
    from_left = piece
    from_right = piece
    for d in range(1, size // 2 + 1):
        from_left = lax.ppermute(from_left, name, left)
        got[-d % size] = from_left
        if d < size - d:
            from_right = lax.ppermute(from_right, name, right)
            got[d] = from_right
    return jnp.stack([got[m] for m in range(size)])


def ring_gather(piece, name, size):
    left = [(i, (i + 1) % size) for i in range(size)]
    right = [(i, (i - 1) % size) for i in range(size)]
    got = {0: piece}
    from_left = piece
    from_right = piece
    for d in range(1, size // 2 + 1):
        from_left = lax.ppermute(from_left, name, left)
        got[-d % size] = from_left
        if d < size - d:
            from_right = lax.ppermute(from_right, name, right)
            got[d] = from_right
    return jnp.stack([got[m] for m in range(size)])


def on_device(
    x_first, x_second, stale_kv, w_qkv, w_out, q_gain, k_gain, layout, counts, slot_block
):
    me = lax.axis_index(PIPE)
    n_seq = math.prod(s for _, s in SEQ_PARTS)
    tokens = BPM * BLOCK
    heads = w_qkv.shape[2] // HS
    width = heads * HS
    scale = 1.0 / math.sqrt(HS)
    linked = slot_mask(layout, counts, slot_block)
    total_blocks = linked.shape[0]
    block_ids = jnp.arange(total_blocks, dtype=jnp.int32)
    batch_of = block_ids // BPM
    mine = lax.dynamic_slice_in_dim(linked, me * BPM, BPM, 0)
    remote = mine & (batch_of != me)[None, :]

    near = lax.all_gather(stale_kv[None], PIPE[1], axis=0, tiled=True)
    pair, near = lax.optimization_barrier((jnp.stack([x_first, x_second]), near))
    ny = PIPE_PARTS[0][1]
    stale = ring_gather(near, PIPE[0], ny).reshape((-1,) + near.shape[1:])
    ring = (lax.axis_index(PIPE[0]) + jnp.arange(ny, dtype=jnp.int32)) % ny
    order = (ring[:, None] * PIPE_PARTS[1][1] + jnp.arange(PIPE_PARTS[1][1], dtype=jnp.int32)[None, :]).reshape(-1)
    remote_ring = remote[:, order]

    def exchange_rows(x):
        spread = jnp.broadcast_to(x[:, None], (x.shape[0], n_seq) + x.shape[1:])
        return lax.all_to_all(spread, SEQ, 1, 1, tiled=False).reshape(x.shape[0], tokens, -1)

    def project(x):
        raw = jnp.einsum("rd,cdh->crh", x, w_qkv, preferred_element_type=jnp.float32)
        query = normalize(raw[0], q_gain, HS).astype(jnp.bfloat16)
        keys = normalize(raw[1], k_gain, HS).astype(jnp.bfloat16)
        values = raw[2].astype(jnp.bfloat16)
        return (query, keys, values)

    xs = exchange_rows(pair)
    q1, k1, v1 = project(xs[0])
    q2, k2, v2 = project(xs[1])

    near_fresh = lax.all_gather(jnp.stack([k1, v1])[None], PIPE[1], axis=0, tiled=True)
    fresh_kv = ring_gather(near_fresh, PIPE[0], ny).reshape((-1,) + near_fresh.shape[1:])

    def attend(query, keys, values, kv, remote):
        allowed = remote[0].astype(jnp.int32)
        attn = block_attend(allowed, query, keys, values, kv, scale)
        part = jnp.dot(attn, w_out, preferred_element_type=jnp.float32).astype(jnp.bfloat16)
        sent = lax.all_to_all(part.reshape(n_seq, tokens // n_seq, -1), SEQ, 0, 0, tiled=False)
        return jnp.sum(sent.astype(jnp.float32), axis=0).astype(jnp.bfloat16)

    out_first = attend(q1, k1, v1, stale, remote_ring)
    out_first, fresh_kv = lax.optimization_barrier((out_first, fresh_kv))
    out_second = attend(q2, k2, v2, fresh_kv, remote_ring)
    return (out_first, out_second)


def solution(mesh):
    names = PIPE_PARTS + SEQ_PARTS
    fine = Mesh(
        np.asarray(mesh.devices).reshape([s for _, s in names]), tuple(n for n, _ in names)
    )
    rows = P(PIPE + SEQ, None)
    placed = (
        rows,
        rows,
        P(None, PIPE, SEQ),
        P(None, None, SEQ),
        P(SEQ, None),
        P(SEQ),
        P(SEQ),
        P(),
        P(),
        P(),
    )
    return jax.shard_map(
        on_device,
        mesh=fine,
        in_specs=placed,
        out_specs=(rows, rows),
        check_vma=False,
    )
```

```python
import functools
import math

import jax
import jax.numpy as jnp
import numpy as np
from jax import lax
from jax.experimental import pallas as pl
from jax.experimental.pallas import tpu as pltpu
from jax.sharding import Mesh
from jax.sharding import PartitionSpec as P

HS = 64
BLOCK = 128
BPM = 1


HIGH = lax.Precision.HIGHEST
NEG = -1e30

PIPE_PARTS = (("y", 8), ("zl", 4))
SEQ_PARTS = (("zh", 2), ("x", 4), ("c", 2))
PIPE = tuple(n for n, _ in PIPE_PARTS)
SEQ = tuple(n for n, _ in SEQ_PARTS)


def slot_mask(layout, counts, slot_block):
    total = layout.shape[0]
    width = layout.shape[1]
    blocks = jnp.arange(total, dtype=jnp.int32)
    valid = jnp.arange(width, dtype=jnp.int32)[None, :] < counts[:, None]
    member = jnp.sum(
        ((layout[:, :, None] == blocks[None, None, :]) & valid[:, :, None]).astype(jnp.float32),
        axis=1,
    )
    placed = (slot_block[:, None] == blocks[None, :]).astype(jnp.float32)
    linked = jnp.dot(jnp.dot(placed, member, precision=HIGH), placed.T, precision=HIGH)
    return linked > 0.5


def normalize(raw, gain, size):
    count = raw.shape[0]
    grid = raw.reshape(count, -1, size)
    factor = lax.rsqrt(jnp.mean(grid * grid, axis=2, keepdims=True) + 1e-06)
    return (grid * factor).reshape(count, -1) * gain[None, :]


def attn_kernel(count_ref, listed_ref, q_ref, k_ref, v_ref, kv_ref, o_ref, *, scale):
    q = q_ref[...] * jnp.asarray(scale, q_ref.dtype)
    rows, width = q.shape
    lane = lax.broadcasted_iota(jnp.int32, (rows, width), 1)
    zero = jnp.zeros_like(q)
    qt0 = jnp.where(lane < HS, q, zero).T
    qt1 = jnp.where(lane < HS, zero, q).T
    first = lax.broadcasted_iota(jnp.int32, (width, rows), 0) < HS

    def update(carry, kb, vb):
        m0, m1, l0, l1, acc = carry
        s0 = jnp.dot(kb, qt0, preferred_element_type=jnp.float32)
        s1 = jnp.dot(kb, qt1, preferred_element_type=jnp.float32)
        n0 = jnp.maximum(m0, jnp.max(s0, axis=0, keepdims=True))
        n1 = jnp.maximum(m1, jnp.max(s1, axis=0, keepdims=True))
        a0 = jnp.exp(m0 - n0)
        a1 = jnp.exp(m1 - n1)
        p0 = jnp.exp(s0 - n0)
        p1 = jnp.exp(s1 - n1)
        l0 = l0 * a0 + jnp.sum(p0, axis=0, keepdims=True)
        l1 = l1 * a1 + jnp.sum(p1, axis=0, keepdims=True)
        vt = vb.T
        pv0 = jnp.dot(vt, p0.astype(vb.dtype), preferred_element_type=jnp.float32)
        pv1 = jnp.dot(vt, p1.astype(vb.dtype), preferred_element_type=jnp.float32)
        acc = acc * jnp.where(first, a0, a1) + jnp.where(first, pv0, pv1)
        return (n0, n1, l0, l1, acc)

    init = (
        jnp.full((1, rows), NEG, jnp.float32),
        jnp.full((1, rows), NEG, jnp.float32),
        jnp.zeros((1, rows), jnp.float32),
        jnp.zeros((1, rows), jnp.float32),
        jnp.zeros((width, rows), jnp.float32),
    )
    carry = update(init, k_ref[...], v_ref[...])

    def body(i, carry):
        b = listed_ref[i]
        return update(carry, kv_ref[b, 0], kv_ref[b, 1])

    m0, m1, l0, l1, acc = lax.fori_loop(0, count_ref[0], body, carry)
    o_ref[...] = (acc / jnp.where(first, l0, l1)).T.astype(o_ref.dtype)


def block_attend(allowed, query, keys, values, kv, scale):
    listed = jnp.argsort(jnp.logical_not(allowed), stable=True).astype(jnp.int32)
    count = jnp.sum(allowed.astype(jnp.int32)).reshape(1)
    smem = pltpu.MemorySpace.SMEM
    vmem = pltpu.MemorySpace.VMEM
    return pl.pallas_call(
        functools.partial(attn_kernel, scale=scale),
        out_shape=jax.ShapeDtypeStruct(query.shape, jnp.bfloat16),
        in_specs=[pl.BlockSpec(memory_space=smem)] * 2 + [pl.BlockSpec(memory_space=vmem)] * 4,
        out_specs=pl.BlockSpec(memory_space=vmem),
    )(count, listed, query, keys, values, kv)


def gather_pipe(piece, order):
    for name in order:
        piece = lax.all_gather(piece, name, axis=0, tiled=True)
    return piece


def on_device(
    x_first, x_second, stale_kv, w_qkv, w_out, q_gain, k_gain, layout, counts, slot_block
):
    me = lax.axis_index(PIPE)
    n_seq = math.prod(s for _, s in SEQ_PARTS)
    tokens = BPM * BLOCK
    heads = w_qkv.shape[2] // HS
    width = heads * HS
    scale = 1.0 / math.sqrt(HS)
    linked = slot_mask(layout, counts, slot_block)
    total_blocks = linked.shape[0]
    block_ids = jnp.arange(total_blocks, dtype=jnp.int32)
    batch_of = block_ids // BPM
    mine = lax.dynamic_slice_in_dim(linked, me * BPM, BPM, 0)
    remote = mine & (batch_of != me)[None, :]

    near = lax.all_gather(stale_kv[None], PIPE[1], axis=0, tiled=True)
    pair, near = lax.optimization_barrier((jnp.stack([x_first, x_second]), near))
    stale = lax.all_gather(near, PIPE[0], axis=0, tiled=True)

    def exchange_rows(x):
        spread = jnp.broadcast_to(x[:, None], (x.shape[0], n_seq) + x.shape[1:])
        return lax.all_to_all(spread, SEQ, 1, 1, tiled=False).reshape(x.shape[0], tokens, -1)

    def project(x):
        raw = jnp.einsum("rd,cdh->crh", x, w_qkv, preferred_element_type=jnp.float32)
        query = normalize(raw[0], q_gain, HS).astype(jnp.bfloat16)
        keys = normalize(raw[1], k_gain, HS).astype(jnp.bfloat16)
        values = raw[2].astype(jnp.bfloat16)
        return (query, keys, values)

    xs = exchange_rows(pair)
    q1, k1, v1 = project(xs[0])
    q2, k2, v2 = project(xs[1])

    fresh_kv = gather_pipe(jnp.stack([k1, v1])[None], tuple(reversed(PIPE)))

    def attend(query, keys, values, kv, remote):
        attn = block_attend(remote[0], query, keys, values, kv, scale)
        part = jnp.dot(attn, w_out, preferred_element_type=jnp.float32).astype(jnp.bfloat16)
        sent = lax.all_to_all(part.reshape(n_seq, tokens // n_seq, -1), SEQ, 0, 0, tiled=False)
        return jnp.sum(sent.astype(jnp.float32), axis=0).astype(jnp.bfloat16)

    out_first = attend(q1, k1, v1, stale, remote)
    out_first, fresh_kv = lax.optimization_barrier((out_first, fresh_kv))
    out_second = attend(q2, k2, v2, fresh_kv, remote)
    return (out_first, out_second)


def solution(mesh):
    names = PIPE_PARTS + SEQ_PARTS
    fine = Mesh(
        np.asarray(mesh.devices).reshape([s for _, s in names]), tuple(n for n, _ in names)
    )
    rows = P(PIPE + SEQ, None)
    placed = (
        rows,
        rows,
        P(None, PIPE, SEQ),
        P(None, None, SEQ),
        P(SEQ, None),
        P(SEQ),
        P(SEQ),
        P(),
        P(),
        P(),
    )
    return jax.shard_map(
        on_device,
        mesh=fine,
        in_specs=placed,
        out_specs=(rows, rows),
        check_vma=False,
    )
```

```python
import functools
import math

import jax
import jax.numpy as jnp
import numpy as np
from jax import lax
from jax.experimental import pallas as pl
from jax.experimental.pallas import tpu as pltpu
from jax.sharding import Mesh
from jax.sharding import PartitionSpec as P

HS = 64
BLOCK = 128
BPM = 1


HIGH = lax.Precision.HIGHEST
NEG = -1e30

PIPE_PARTS = (("y", 8), ("zl", 4))
SEQ_PARTS = (("zh", 2), ("x", 4), ("c", 2))
PIPE = tuple(n for n, _ in PIPE_PARTS)
SEQ = tuple(n for n, _ in SEQ_PARTS)


def slot_mask(layout, counts, slot_block):
    total = layout.shape[0]
    width = layout.shape[1]
    blocks = jnp.arange(total, dtype=jnp.int32)
    valid = jnp.arange(width, dtype=jnp.int32)[None, :] < counts[:, None]
    member = jnp.sum(
        ((layout[:, :, None] == blocks[None, None, :]) & valid[:, :, None]).astype(jnp.float32),
        axis=1,
    )
    placed = (slot_block[:, None] == blocks[None, :]).astype(jnp.float32)
    linked = jnp.dot(jnp.dot(placed, member, precision=HIGH), placed.T, precision=HIGH)
    return linked > 0.5


def normalize(raw, gain, size):
    count = raw.shape[0]
    grid = raw.reshape(count, -1, size)
    factor = lax.rsqrt(jnp.mean(grid * grid, axis=2, keepdims=True) + 1e-06)
    return (grid * factor).reshape(count, -1) * gain[None, :]


def attn_kernel(count_ref, listed_ref, q_ref, k_ref, v_ref, kv_ref, o_ref, *, scale):
    q = q_ref[...] * jnp.asarray(scale, q_ref.dtype)
    rows, width = q.shape
    lane = lax.broadcasted_iota(jnp.int32, (rows, width), 1)
    zero = jnp.zeros_like(q)
    both = jnp.concatenate([jnp.where(lane < HS, q, zero).T, jnp.where(lane < HS, zero, q).T], axis=1)
    first = lax.broadcasted_iota(jnp.int32, (width, rows), 0) < HS

    def update(carry, kb, vb):
        m, l, acc = carry
        s = jnp.dot(kb, both, preferred_element_type=jnp.float32)
        n = jnp.maximum(m, jnp.max(s, axis=0, keepdims=True))
        a = jnp.exp(m - n)
        p = jnp.exp(s - n)
        l = l * a + jnp.sum(p, axis=0, keepdims=True)
        pv = jnp.dot(vb.T, p.astype(vb.dtype), preferred_element_type=jnp.float32)
        scaled = jnp.where(first, a[:, :rows], a[:, rows:])
        acc = acc * scaled + jnp.where(first, pv[:, :rows], pv[:, rows:])
        return (n, l, acc)

    init = (
        jnp.full((1, 2 * rows), NEG, jnp.float32),
        jnp.zeros((1, 2 * rows), jnp.float32),
        jnp.zeros((width, rows), jnp.float32),
    )
    carry = update(init, k_ref[...], v_ref[...])

    def body(i, carry):
        b = listed_ref[i]
        return update(carry, kv_ref[b, 0], kv_ref[b, 1])

    m, l, acc = lax.fori_loop(0, count_ref[0], body, carry)
    o_ref[...] = (acc / jnp.where(first, l[:, :rows], l[:, rows:])).T.astype(o_ref.dtype)


def block_attend(allowed, query, keys, values, kv, scale):
    listed = jnp.argsort(jnp.logical_not(allowed), stable=True).astype(jnp.int32)
    count = jnp.sum(allowed.astype(jnp.int32)).reshape(1)
    smem = pltpu.MemorySpace.SMEM
    vmem = pltpu.MemorySpace.VMEM
    return pl.pallas_call(
        functools.partial(attn_kernel, scale=scale),
        out_shape=jax.ShapeDtypeStruct(query.shape, jnp.bfloat16),
        in_specs=[pl.BlockSpec(memory_space=smem)] * 2 + [pl.BlockSpec(memory_space=vmem)] * 4,
        out_specs=pl.BlockSpec(memory_space=vmem),
    )(count, listed, query, keys, values, kv)


def gather_pipe(piece, order):
    for name in order:
        piece = lax.all_gather(piece, name, axis=0, tiled=True)
    return piece


def on_device(
    x_first, x_second, stale_kv, w_qkv, w_out, q_gain, k_gain, layout, counts, slot_block
):
    me = lax.axis_index(PIPE)
    n_seq = math.prod(s for _, s in SEQ_PARTS)
    tokens = BPM * BLOCK
    heads = w_qkv.shape[2] // HS
    width = heads * HS
    scale = 1.0 / math.sqrt(HS)
    linked = slot_mask(layout, counts, slot_block)
    total_blocks = linked.shape[0]
    block_ids = jnp.arange(total_blocks, dtype=jnp.int32)
    batch_of = block_ids // BPM
    mine = lax.dynamic_slice_in_dim(linked, me * BPM, BPM, 0)
    remote = mine & (batch_of != me)[None, :]

    near = lax.all_gather(stale_kv[None], PIPE[1], axis=0, tiled=True)
    pair, near = lax.optimization_barrier((jnp.stack([x_first, x_second]), near))
    stale = lax.all_gather(near, PIPE[0], axis=0, tiled=True)

    def exchange_rows(x):
        spread = jnp.broadcast_to(x[:, None], (x.shape[0], n_seq) + x.shape[1:])
        return lax.all_to_all(spread, SEQ, 1, 1, tiled=False).reshape(x.shape[0], tokens, -1)

    def project(x):
        raw = jnp.einsum("rd,cdh->crh", x, w_qkv, preferred_element_type=jnp.float32)
        query = normalize(raw[0], q_gain, HS).astype(jnp.bfloat16)
        keys = normalize(raw[1], k_gain, HS).astype(jnp.bfloat16)
        values = raw[2].astype(jnp.bfloat16)
        return (query, keys, values)

    xs = exchange_rows(pair)
    q1, k1, v1 = project(xs[0])
    q2, k2, v2 = project(xs[1])

    fresh_kv = gather_pipe(jnp.stack([k1, v1])[None], tuple(reversed(PIPE)))

    def attend(query, keys, values, kv, remote):
        attn = block_attend(remote[0], query, keys, values, kv, scale)
        part = jnp.dot(attn, w_out, preferred_element_type=jnp.float32).astype(jnp.bfloat16)
        sent = lax.all_to_all(part.reshape(n_seq, tokens // n_seq, -1), SEQ, 0, 0, tiled=False)
        return jnp.sum(sent.astype(jnp.float32), axis=0).astype(jnp.bfloat16)

    out_first = attend(q1, k1, v1, stale, remote)
    out_first, fresh_kv = lax.optimization_barrier((out_first, fresh_kv))
    out_second = attend(q2, k2, v2, fresh_kv, remote)
    return (out_first, out_second)


def solution(mesh):
    names = PIPE_PARTS + SEQ_PARTS
    fine = Mesh(
        np.asarray(mesh.devices).reshape([s for _, s in names]), tuple(n for n, _ in names)
    )
    rows = P(PIPE + SEQ, None)
    placed = (
        rows,
        rows,
        P(None, PIPE, SEQ),
        P(None, None, SEQ),
        P(SEQ, None),
        P(SEQ),
        P(SEQ),
        P(),
        P(),
        P(),
    )
    return jax.shard_map(
        on_device,
        mesh=fine,
        in_specs=placed,
        out_specs=(rows, rows),
        check_vma=False,
    )
```

```python
import functools
import math

import jax
import jax.numpy as jnp
import numpy as np
from jax import lax
from jax.experimental import pallas as pl
from jax.experimental.pallas import tpu as pltpu
from jax.sharding import Mesh
from jax.sharding import PartitionSpec as P

HS = 64
BLOCK = 128
BPM = 1


HIGH = lax.Precision.HIGHEST
NEG = -1e30

PIPE_PARTS = (("y", 8), ("zl", 4))
SEQ_PARTS = (("zh", 2), ("x", 4), ("c", 2))
PIPE = tuple(n for n, _ in PIPE_PARTS)
SEQ = tuple(n for n, _ in SEQ_PARTS)


def slot_mask(layout, counts, slot_block):
    total = layout.shape[0]
    width = layout.shape[1]
    blocks = jnp.arange(total, dtype=jnp.int32)
    valid = jnp.arange(width, dtype=jnp.int32)[None, :] < counts[:, None]
    member = jnp.sum(
        ((layout[:, :, None] == blocks[None, None, :]) & valid[:, :, None]).astype(jnp.float32),
        axis=1,
    )
    placed = (slot_block[:, None] == blocks[None, :]).astype(jnp.float32)
    linked = jnp.dot(jnp.dot(placed, member, precision=HIGH), placed.T, precision=HIGH)
    return linked > 0.5


def normalize(raw, gain, size):
    count = raw.shape[0]
    grid = raw.reshape(count, -1, size)
    factor = lax.rsqrt(jnp.mean(grid * grid, axis=2, keepdims=True) + 1e-06)
    return (grid * factor).reshape(count, -1) * gain[None, :]


def attn_kernel(allowed_ref, q_ref, k_ref, v_ref, kv_ref, o_ref, *, scale, n_blocks):
    q = q_ref[...] * jnp.asarray(scale, q_ref.dtype)
    rows, width = q.shape
    lane = lax.broadcasted_iota(jnp.int32, (rows, width), 1)
    zero = jnp.zeros_like(q)
    qt0 = jnp.where(lane < HS, q, zero).T
    qt1 = jnp.where(lane < HS, zero, q).T
    first = lax.broadcasted_iota(jnp.int32, (width, rows), 0) < HS

    def update(carry, kb, vb):
        m0, m1, l0, l1, acc = carry
        s0 = jnp.dot(kb, qt0, preferred_element_type=jnp.float32)
        s1 = jnp.dot(kb, qt1, preferred_element_type=jnp.float32)
        n0 = jnp.maximum(m0, jnp.max(s0, axis=0, keepdims=True))
        n1 = jnp.maximum(m1, jnp.max(s1, axis=0, keepdims=True))
        a0 = jnp.exp(m0 - n0)
        a1 = jnp.exp(m1 - n1)
        p0 = jnp.exp(s0 - n0)
        p1 = jnp.exp(s1 - n1)
        l0 = l0 * a0 + jnp.sum(p0, axis=0, keepdims=True)
        l1 = l1 * a1 + jnp.sum(p1, axis=0, keepdims=True)
        vt = vb.T
        pv0 = jnp.dot(vt, p0.astype(vb.dtype), preferred_element_type=jnp.float32)
        pv1 = jnp.dot(vt, p1.astype(vb.dtype), preferred_element_type=jnp.float32)
        acc = acc * jnp.where(first, a0, a1) + jnp.where(first, pv0, pv1)
        return (n0, n1, l0, l1, acc)

    init = (
        jnp.full((1, rows), NEG, jnp.float32),
        jnp.full((1, rows), NEG, jnp.float32),
        jnp.zeros((1, rows), jnp.float32),
        jnp.zeros((1, rows), jnp.float32),
        jnp.zeros((width, rows), jnp.float32),
    )
    carry = update(init, k_ref[...], v_ref[...])

    def visit(b, carry):
        return update(carry, kv_ref[b, 0], kv_ref[b, 1])

    def body(b, carry):
        return lax.cond(allowed_ref[b] > 0, functools.partial(visit, b), lambda c: c, carry)

    m0, m1, l0, l1, acc = lax.fori_loop(0, n_blocks, body, carry)
    o_ref[...] = (acc / jnp.where(first, l0, l1)).T.astype(o_ref.dtype)


def block_attend(allowed, query, keys, values, kv, scale):
    n_blocks = kv.shape[0]
    vmem = pltpu.MemorySpace.VMEM
    return pl.pallas_call(
        functools.partial(attn_kernel, scale=scale, n_blocks=n_blocks),
        out_shape=jax.ShapeDtypeStruct(query.shape, jnp.bfloat16),
        in_specs=[pl.BlockSpec(memory_space=pltpu.MemorySpace.SMEM)] + [pl.BlockSpec(memory_space=vmem)] * 4,
        out_specs=pl.BlockSpec(memory_space=vmem),
    )(allowed, query, keys, values, kv)


def gather_pipe(piece, order):
    for name in order:
        piece = lax.all_gather(piece, name, axis=0, tiled=True)
    return piece


def on_device(
    x_first, x_second, stale_kv, w_qkv, w_out, q_gain, k_gain, layout, counts, slot_block
):
    me = lax.axis_index(PIPE)
    n_seq = math.prod(s for _, s in SEQ_PARTS)
    tokens = BPM * BLOCK
    heads = w_qkv.shape[2] // HS
    width = heads * HS
    scale = 1.0 / math.sqrt(HS)
    linked = slot_mask(layout, counts, slot_block)
    total_blocks = linked.shape[0]
    block_ids = jnp.arange(total_blocks, dtype=jnp.int32)
    batch_of = block_ids // BPM
    mine = lax.dynamic_slice_in_dim(linked, me * BPM, BPM, 0)
    remote = mine & (batch_of != me)[None, :]

    near = lax.all_gather(stale_kv[None], PIPE[1], axis=0, tiled=True)
    pair, near = lax.optimization_barrier((jnp.stack([x_first, x_second]), near))
    stale = lax.all_gather(near, PIPE[0], axis=0, tiled=True)

    def exchange_rows(x):
        spread = jnp.broadcast_to(x[:, None], (x.shape[0], n_seq) + x.shape[1:])
        return lax.all_to_all(spread, SEQ, 1, 1, tiled=False).reshape(x.shape[0], tokens, -1)

    def project(x):
        raw = jnp.einsum("rd,cdh->crh", x, w_qkv, preferred_element_type=jnp.float32)
        query = normalize(raw[0], q_gain, HS).astype(jnp.bfloat16)
        keys = normalize(raw[1], k_gain, HS).astype(jnp.bfloat16)
        values = raw[2].astype(jnp.bfloat16)
        return (query, keys, values)

    xs = exchange_rows(pair)
    q1, k1, v1 = project(xs[0])
    q2, k2, v2 = project(xs[1])

    fresh_kv = gather_pipe(jnp.stack([k1, v1])[None], tuple(reversed(PIPE)))

    def attend(query, keys, values, kv, remote):
        allowed = remote[0].astype(jnp.int32)
        attn = block_attend(allowed, query, keys, values, kv, scale)
        part = jnp.dot(attn, w_out, preferred_element_type=jnp.float32).astype(jnp.bfloat16)
        chip = SEQ_PARTS[-1][1]
        split = part.reshape(n_seq // chip, chip, tokens // n_seq, -1)
        pair_sum = jnp.sum(lax.all_to_all(split, SEQ[-1], 1, 1, tiled=False).astype(jnp.float32), axis=1)
        sent = lax.all_to_all(pair_sum.astype(jnp.bfloat16), SEQ[:-1], 0, 0, tiled=False)
        return jnp.sum(sent.astype(jnp.float32), axis=0).astype(jnp.bfloat16)

    out_first = attend(q1, k1, v1, stale, remote)
    out_first, fresh_kv = lax.optimization_barrier((out_first, fresh_kv))
    out_second = attend(q2, k2, v2, fresh_kv, remote)
    return (out_first, out_second)


def solution(mesh):
    names = PIPE_PARTS + SEQ_PARTS
    fine = Mesh(
        np.asarray(mesh.devices).reshape([s for _, s in names]), tuple(n for n, _ in names)
    )
    rows = P(PIPE + SEQ, None)
    placed = (
        rows,
        rows,
        P(None, PIPE, SEQ),
        P(None, None, SEQ),
        P(SEQ, None),
        P(SEQ),
        P(SEQ),
        P(),
        P(),
        P(),
    )
    return jax.shard_map(
        on_device,
        mesh=fine,
        in_specs=placed,
        out_specs=(rows, rows),
        check_vma=False,
    )
```

```python
import functools
import math

import jax
import jax.numpy as jnp
import numpy as np
from jax import lax
from jax.experimental import pallas as pl
from jax.experimental.pallas import tpu as pltpu
from jax.sharding import Mesh
from jax.sharding import PartitionSpec as P

HS = 64
BLOCK = 128
BPM = 1


HIGH = lax.Precision.HIGHEST
NEG = -1e30

PIPE_PARTS = (("y", 8), ("zl", 4))
SEQ_PARTS = (("zh", 2), ("x", 4), ("c", 2))
PIPE = tuple(n for n, _ in PIPE_PARTS)
SEQ = tuple(n for n, _ in SEQ_PARTS)


def slot_mask(layout, counts, slot_block):
    total = layout.shape[0]
    width = layout.shape[1]
    blocks = jnp.arange(total, dtype=jnp.int32)
    valid = jnp.arange(width, dtype=jnp.int32)[None, :] < counts[:, None]
    member = jnp.sum(
        ((layout[:, :, None] == blocks[None, None, :]) & valid[:, :, None]).astype(jnp.float32),
        axis=1,
    )
    placed = (slot_block[:, None] == blocks[None, :]).astype(jnp.float32)
    linked = jnp.dot(jnp.dot(placed, member, precision=HIGH), placed.T, precision=HIGH)
    return linked > 0.5


def normalize(raw, gain, size):
    count = raw.shape[0]
    grid = raw.reshape(count, -1, size)
    factor = lax.rsqrt(jnp.mean(grid * grid, axis=2, keepdims=True) + 1e-06)
    return (grid * factor).reshape(count, -1) * gain[None, :]


def attn_kernel(allowed_ref, q_ref, k_ref, v_ref, kv_ref, o_ref, *, scale, n_blocks):
    q = q_ref[...] * jnp.asarray(scale, q_ref.dtype)
    rows, width = q.shape
    lane = lax.broadcasted_iota(jnp.int32, (rows, width), 1)
    zero = jnp.zeros_like(q)
    qt0 = jnp.where(lane < HS, q, zero).T
    qt1 = jnp.where(lane < HS, zero, q).T
    first = lax.broadcasted_iota(jnp.int32, (width, rows), 0) < HS

    def update(carry, kb, vb):
        m0, m1, l0, l1, acc = carry
        s0 = jnp.dot(kb, qt0, preferred_element_type=jnp.float32)
        s1 = jnp.dot(kb, qt1, preferred_element_type=jnp.float32)
        n0 = jnp.maximum(m0, jnp.max(s0, axis=0, keepdims=True))
        n1 = jnp.maximum(m1, jnp.max(s1, axis=0, keepdims=True))
        a0 = jnp.exp(m0 - n0)
        a1 = jnp.exp(m1 - n1)
        p0 = jnp.exp(s0 - n0)
        p1 = jnp.exp(s1 - n1)
        l0 = l0 * a0 + jnp.sum(p0, axis=0, keepdims=True)
        l1 = l1 * a1 + jnp.sum(p1, axis=0, keepdims=True)
        vt = vb.T
        pv0 = jnp.dot(vt, p0.astype(vb.dtype), preferred_element_type=jnp.float32)
        pv1 = jnp.dot(vt, p1.astype(vb.dtype), preferred_element_type=jnp.float32)
        acc = acc * jnp.where(first, a0, a1) + jnp.where(first, pv0, pv1)
        return (n0, n1, l0, l1, acc)

    init = (
        jnp.full((1, rows), NEG, jnp.float32),
        jnp.full((1, rows), NEG, jnp.float32),
        jnp.zeros((1, rows), jnp.float32),
        jnp.zeros((1, rows), jnp.float32),
        jnp.zeros((width, rows), jnp.float32),
    )
    carry = update(init, k_ref[...], v_ref[...])

    def visit(b, carry):
        return update(carry, kv_ref[b, 0], kv_ref[b, 1])

    def body(b, carry):
        return lax.cond(allowed_ref[b] > 0, functools.partial(visit, b), lambda c: c, carry)

    m0, m1, l0, l1, acc = lax.fori_loop(0, n_blocks, body, carry)
    o_ref[...] = (acc / jnp.where(first, l0, l1)).T.astype(o_ref.dtype)


def block_attend(allowed, query, keys, values, kv, scale):
    n_blocks = kv.shape[0]
    vmem = pltpu.MemorySpace.VMEM
    return pl.pallas_call(
        functools.partial(attn_kernel, scale=scale, n_blocks=n_blocks),
        out_shape=jax.ShapeDtypeStruct(query.shape, jnp.bfloat16),
        in_specs=[pl.BlockSpec(memory_space=pltpu.MemorySpace.SMEM)] + [pl.BlockSpec(memory_space=vmem)] * 4,
        out_specs=pl.BlockSpec(memory_space=vmem),
    )(allowed, query, keys, values, kv)


def gather_pipe(piece, order):
    for name in order:
        piece = lax.all_gather(piece, name, axis=0, tiled=True)
    return piece


def on_device(
    x_first, x_second, stale_kv, w_qkv, w_out, q_gain, k_gain, layout, counts, slot_block
):
    me = lax.axis_index(PIPE)
    n_seq = math.prod(s for _, s in SEQ_PARTS)
    tokens = BPM * BLOCK
    heads = w_qkv.shape[2] // HS
    width = heads * HS
    scale = 1.0 / math.sqrt(HS)
    linked = slot_mask(layout, counts, slot_block)
    total_blocks = linked.shape[0]
    block_ids = jnp.arange(total_blocks, dtype=jnp.int32)
    batch_of = block_ids // BPM
    mine = lax.dynamic_slice_in_dim(linked, me * BPM, BPM, 0)
    remote = mine & (batch_of != me)[None, :]

    near = lax.all_gather(stale_kv[None], PIPE[1], axis=0, tiled=True)
    pair, near = lax.optimization_barrier((jnp.stack([x_first, x_second]), near))
    stale = lax.all_gather(near, PIPE[0], axis=0, tiled=True)

    chip = SEQ_PARTS[-1][1]

    def exchange_rows(x):
        steps = x.shape[0]
        spread = jnp.broadcast_to(x[:, None], (steps, n_seq // chip) + x.shape[1:])
        among = lax.all_to_all(spread, SEQ[:-1], 1, 1, tiled=False)
        spread = jnp.broadcast_to(among[:, None], (steps, chip) + among.shape[1:])
        return lax.all_to_all(spread, SEQ[-1], 1, 1, tiled=False).reshape(steps, tokens, -1)

    def project(x):
        raw = jnp.einsum("rd,cdh->crh", x, w_qkv, preferred_element_type=jnp.float32)
        query = normalize(raw[0], q_gain, HS).astype(jnp.bfloat16)
        keys = normalize(raw[1], k_gain, HS).astype(jnp.bfloat16)
        values = raw[2].astype(jnp.bfloat16)
        return (query, keys, values)

    xs = exchange_rows(pair)
    q1, k1, v1 = project(xs[0])
    q2, k2, v2 = project(xs[1])

    fresh_kv = gather_pipe(jnp.stack([k1, v1])[None], tuple(reversed(PIPE)))

    def attend(query, keys, values, kv, remote):
        allowed = remote[0].astype(jnp.int32)
        attn = block_attend(allowed, query, keys, values, kv, scale)
        part = jnp.dot(attn, w_out, preferred_element_type=jnp.float32).astype(jnp.bfloat16)
        split = part.reshape(chip, n_seq // chip, tokens // n_seq, -1)
        pair_sum = jnp.sum(lax.all_to_all(split, SEQ[-1], 0, 0, tiled=False).astype(jnp.float32), axis=0)
        sent = lax.all_to_all(pair_sum.astype(jnp.bfloat16), SEQ[:-1], 0, 0, tiled=False)
        return jnp.sum(sent.astype(jnp.float32), axis=0).astype(jnp.bfloat16)

    out_first = attend(q1, k1, v1, stale, remote)
    out_first, fresh_kv = lax.optimization_barrier((out_first, fresh_kv))
    out_second = attend(q2, k2, v2, fresh_kv, remote)
    return (out_first, out_second)


def solution(mesh):
    names = PIPE_PARTS + SEQ_PARTS
    fine = Mesh(
        np.asarray(mesh.devices).reshape([s for _, s in names]), tuple(n for n, _ in names)
    )
    rows = P(PIPE + SEQ, None)
    placed = (
        rows,
        rows,
        P(None, PIPE, SEQ),
        P(None, None, SEQ),
        P(SEQ, None),
        P(SEQ),
        P(SEQ),
        P(),
        P(),
        P(),
    )
    return jax.shard_map(
        on_device,
        mesh=fine,
        in_specs=placed,
        out_specs=(rows, rows),
        check_vma=False,
    )
```

```python
import functools
import math

import jax
import jax.numpy as jnp
import numpy as np
from jax import lax
from jax.experimental import pallas as pl
from jax.experimental.pallas import tpu as pltpu
from jax.sharding import Mesh
from jax.sharding import PartitionSpec as P

HS = 64
BLOCK = 128
BPM = 1


HIGH = lax.Precision.HIGHEST
NEG = -1e30

PIPE_PARTS = (("y", 8), ("zl", 4))
SEQ_PARTS = (("zh", 2), ("x", 4), ("c", 2))
PIPE = tuple(n for n, _ in PIPE_PARTS)
SEQ = tuple(n for n, _ in SEQ_PARTS)


def slot_mask(layout, counts, slot_block):
    total = layout.shape[0]
    width = layout.shape[1]
    blocks = jnp.arange(total, dtype=jnp.int32)
    valid = jnp.arange(width, dtype=jnp.int32)[None, :] < counts[:, None]
    member = jnp.sum(
        ((layout[:, :, None] == blocks[None, None, :]) & valid[:, :, None]).astype(jnp.float32),
        axis=1,
    )
    placed = (slot_block[:, None] == blocks[None, :]).astype(jnp.float32)
    linked = jnp.dot(jnp.dot(placed, member, precision=HIGH), placed.T, precision=HIGH)
    return linked > 0.5


def normalize(raw, gain, size):
    count = raw.shape[0]
    grid = raw.reshape(count, -1, size)
    factor = lax.rsqrt(jnp.mean(grid * grid, axis=2, keepdims=True) + 1e-06)
    return (grid * factor).reshape(count, -1) * gain[None, :]


def attn_kernel(allowed_ref, q_ref, k_ref, v_ref, kv_ref, o_ref, *, scale, n_blocks):
    q = q_ref[...] * jnp.asarray(scale, q_ref.dtype)
    rows, width = q.shape
    lane = lax.broadcasted_iota(jnp.int32, (rows, width), 1)
    zero = jnp.zeros_like(q)
    qt0 = jnp.where(lane < HS, q, zero).T
    qt1 = jnp.where(lane < HS, zero, q).T
    first = lax.broadcasted_iota(jnp.int32, (width, rows), 0) < HS

    def update(carry, kb, vb):
        m0, m1, l0, l1, acc = carry
        s0 = jnp.dot(kb, qt0, preferred_element_type=jnp.float32)
        s1 = jnp.dot(kb, qt1, preferred_element_type=jnp.float32)
        n0 = jnp.maximum(m0, jnp.max(s0, axis=0, keepdims=True))
        n1 = jnp.maximum(m1, jnp.max(s1, axis=0, keepdims=True))
        a0 = jnp.exp(m0 - n0)
        a1 = jnp.exp(m1 - n1)
        p0 = jnp.exp(s0 - n0)
        p1 = jnp.exp(s1 - n1)
        l0 = l0 * a0 + jnp.sum(p0, axis=0, keepdims=True)
        l1 = l1 * a1 + jnp.sum(p1, axis=0, keepdims=True)
        vt = vb.T
        pv0 = jnp.dot(vt, p0.astype(vb.dtype), preferred_element_type=jnp.float32)
        pv1 = jnp.dot(vt, p1.astype(vb.dtype), preferred_element_type=jnp.float32)
        acc = acc * jnp.where(first, a0, a1) + jnp.where(first, pv0, pv1)
        return (n0, n1, l0, l1, acc)

    init = (
        jnp.full((1, rows), NEG, jnp.float32),
        jnp.full((1, rows), NEG, jnp.float32),
        jnp.zeros((1, rows), jnp.float32),
        jnp.zeros((1, rows), jnp.float32),
        jnp.zeros((width, rows), jnp.float32),
    )
    carry = update(init, k_ref[...], v_ref[...])

    def visit(b, carry):
        return update(carry, kv_ref[b, 0], kv_ref[b, 1])

    def body(b, carry):
        return lax.cond(allowed_ref[b] > 0, functools.partial(visit, b), lambda c: c, carry)

    m0, m1, l0, l1, acc = lax.fori_loop(0, n_blocks, body, carry)
    o_ref[...] = (acc / jnp.where(first, l0, l1)).T.astype(o_ref.dtype)


def block_attend(allowed, query, keys, values, kv, scale):
    n_blocks = kv.shape[0]
    vmem = pltpu.MemorySpace.VMEM
    return pl.pallas_call(
        functools.partial(attn_kernel, scale=scale, n_blocks=n_blocks),
        out_shape=jax.ShapeDtypeStruct(query.shape, jnp.bfloat16),
        in_specs=[pl.BlockSpec(memory_space=pltpu.MemorySpace.SMEM)] + [pl.BlockSpec(memory_space=vmem)] * 4,
        out_specs=pl.BlockSpec(memory_space=vmem),
    )(allowed, query, keys, values, kv)


def gather_pipe(piece, order):
    for name in order:
        piece = lax.all_gather(piece, name, axis=0, tiled=True)
    return piece


def on_device(
    x_first, x_second, stale_kv, w_qkv, w_out, q_gain, k_gain, layout, counts, slot_block
):
    me = lax.axis_index(PIPE)
    n_seq = math.prod(s for _, s in SEQ_PARTS)
    tokens = BPM * BLOCK
    heads = w_qkv.shape[2] // HS
    width = heads * HS
    scale = 1.0 / math.sqrt(HS)
    linked = slot_mask(layout, counts, slot_block)
    total_blocks = linked.shape[0]
    block_ids = jnp.arange(total_blocks, dtype=jnp.int32)
    batch_of = block_ids // BPM
    mine = lax.dynamic_slice_in_dim(linked, me * BPM, BPM, 0)
    remote = mine & (batch_of != me)[None, :]

    near = lax.all_gather(stale_kv[None], PIPE[1], axis=0, tiled=True)
    pair, near = lax.optimization_barrier((jnp.stack([x_first, x_second]), near))
    stale = lax.all_gather(near, PIPE[0], axis=0, tiled=True)

    chip = SEQ_PARTS[-1][1]

    def exchange_rows(x):
        steps = x.shape[0]
        spread = jnp.broadcast_to(x[:, None], (steps, n_seq // chip) + x.shape[1:])
        among = lax.all_to_all(spread, SEQ[:-1], 1, 1, tiled=False)
        spread = jnp.broadcast_to(among[:, None], (steps, chip) + among.shape[1:])
        return lax.all_to_all(spread, SEQ[-1], 1, 1, tiled=False).reshape(steps, tokens, -1)

    n_proj = w_qkv.shape[0]
    w_all = w_qkv.transpose(1, 0, 2).reshape(w_qkv.shape[1], n_proj * width)
    xs = exchange_rows(pair)
    raw = jnp.dot(xs.reshape(-1, xs.shape[-1]), w_all, preferred_element_type=jnp.float32)
    raw = raw.reshape(xs.shape[0], tokens, n_proj, width)

    def project(raw):
        query = normalize(raw[:, 0], q_gain, HS).astype(jnp.bfloat16)
        keys = normalize(raw[:, 1], k_gain, HS).astype(jnp.bfloat16)
        values = raw[:, 2].astype(jnp.bfloat16)
        return (query, keys, values)

    q1, k1, v1 = project(raw[0])
    q2, k2, v2 = project(raw[1])

    fresh_kv = gather_pipe(jnp.stack([k1, v1])[None], tuple(reversed(PIPE)))

    def attend(query, keys, values, kv, remote):
        allowed = remote[0].astype(jnp.int32)
        attn = block_attend(allowed, query, keys, values, kv, scale)
        part = jnp.dot(attn, w_out, preferred_element_type=jnp.float32).astype(jnp.bfloat16)
        split = part.reshape(chip, n_seq // chip, tokens // n_seq, -1)
        pair_sum = jnp.sum(lax.all_to_all(split, SEQ[-1], 0, 0, tiled=False).astype(jnp.float32), axis=0)
        sent = lax.all_to_all(pair_sum.astype(jnp.bfloat16), SEQ[:-1], 0, 0, tiled=False)
        return jnp.sum(sent.astype(jnp.float32), axis=0).astype(jnp.bfloat16)

    out_first = attend(q1, k1, v1, stale, remote)
    out_first, fresh_kv = lax.optimization_barrier((out_first, fresh_kv))
    out_second = attend(q2, k2, v2, fresh_kv, remote)
    return (out_first, out_second)


def solution(mesh):
    names = PIPE_PARTS + SEQ_PARTS
    fine = Mesh(
        np.asarray(mesh.devices).reshape([s for _, s in names]), tuple(n for n, _ in names)
    )
    rows = P(PIPE + SEQ, None)
    placed = (
        rows,
        rows,
        P(None, PIPE, SEQ),
        P(None, None, SEQ),
        P(SEQ, None),
        P(SEQ),
        P(SEQ),
        P(),
        P(),
        P(),
    )
    return jax.shard_map(
        on_device,
        mesh=fine,
        in_specs=placed,
        out_specs=(rows, rows),
        check_vma=False,
    )
```

```python
import functools
import math

import jax
import jax.numpy as jnp
import numpy as np
from jax import lax
from jax.experimental import pallas as pl
from jax.experimental.pallas import tpu as pltpu
from jax.sharding import Mesh
from jax.sharding import PartitionSpec as P

HS = 64
BLOCK = 128
BPM = 1


HIGH = lax.Precision.HIGHEST
NEG = -1e30

PIPE_PARTS = (("y", 8), ("zl", 4))
SEQ_PARTS = (("zh", 2), ("x", 4), ("c", 2))
PIPE = tuple(n for n, _ in PIPE_PARTS)
SEQ = tuple(n for n, _ in SEQ_PARTS)


def slot_mask(layout, counts, slot_block):
    total = layout.shape[0]
    width = layout.shape[1]
    blocks = jnp.arange(total, dtype=jnp.int32)
    valid = jnp.arange(width, dtype=jnp.int32)[None, :] < counts[:, None]
    member = jnp.sum(
        ((layout[:, :, None] == blocks[None, None, :]) & valid[:, :, None]).astype(jnp.float32),
        axis=1,
    )
    placed = (slot_block[:, None] == blocks[None, :]).astype(jnp.float32)
    linked = jnp.dot(jnp.dot(placed, member, precision=HIGH), placed.T, precision=HIGH)
    return linked > 0.5


def normalize(raw, gain, size):
    count = raw.shape[0]
    grid = raw.reshape(count, -1, size)
    factor = lax.rsqrt(jnp.mean(grid * grid, axis=2, keepdims=True) + 1e-06)
    return (grid * factor).reshape(count, -1) * gain[None, :]


def attn_kernel(allowed_ref, q_ref, k_ref, v_ref, kv_ref, o_ref, *, scale, n_blocks):
    q = q_ref[...] * jnp.asarray(scale, q_ref.dtype)
    rows, width = q.shape
    lane = lax.broadcasted_iota(jnp.int32, (rows, width), 1)
    zero = jnp.zeros_like(q)
    qt0 = jnp.where(lane < HS, q, zero).T
    qt1 = jnp.where(lane < HS, zero, q).T
    first = lax.broadcasted_iota(jnp.int32, (width, rows), 0) < HS

    def update(carry, kb, vb):
        m0, m1, l0, l1, acc = carry
        s0 = jnp.dot(kb, qt0, preferred_element_type=jnp.float32)
        s1 = jnp.dot(kb, qt1, preferred_element_type=jnp.float32)
        n0 = jnp.maximum(m0, jnp.max(s0, axis=0, keepdims=True))
        n1 = jnp.maximum(m1, jnp.max(s1, axis=0, keepdims=True))
        a0 = jnp.exp(m0 - n0)
        a1 = jnp.exp(m1 - n1)
        p0 = jnp.exp(s0 - n0)
        p1 = jnp.exp(s1 - n1)
        l0 = l0 * a0 + jnp.sum(p0, axis=0, keepdims=True)
        l1 = l1 * a1 + jnp.sum(p1, axis=0, keepdims=True)
        vt = vb.T
        pv0 = jnp.dot(vt, p0.astype(vb.dtype), preferred_element_type=jnp.float32)
        pv1 = jnp.dot(vt, p1.astype(vb.dtype), preferred_element_type=jnp.float32)
        acc = acc * jnp.where(first, a0, a1) + jnp.where(first, pv0, pv1)
        return (n0, n1, l0, l1, acc)

    init = (
        jnp.full((1, rows), NEG, jnp.float32),
        jnp.full((1, rows), NEG, jnp.float32),
        jnp.zeros((1, rows), jnp.float32),
        jnp.zeros((1, rows), jnp.float32),
        jnp.zeros((width, rows), jnp.float32),
    )
    carry = update(init, k_ref[...], v_ref[...])

    def visit(b, carry):
        return update(carry, kv_ref[b, 0], kv_ref[b, 1])

    def body(b, carry):
        return lax.cond(allowed_ref[b] > 0, functools.partial(visit, b), lambda c: c, carry)

    m0, m1, l0, l1, acc = lax.fori_loop(0, n_blocks, body, carry)
    o_ref[...] = (acc / jnp.where(first, l0, l1)).T.astype(o_ref.dtype)


def block_attend(allowed, query, keys, values, kv, scale):
    n_blocks = kv.shape[0]
    vmem = pltpu.MemorySpace.VMEM
    return pl.pallas_call(
        functools.partial(attn_kernel, scale=scale, n_blocks=n_blocks),
        out_shape=jax.ShapeDtypeStruct(query.shape, jnp.bfloat16),
        in_specs=[pl.BlockSpec(memory_space=pltpu.MemorySpace.SMEM)] + [pl.BlockSpec(memory_space=vmem)] * 4,
        out_specs=pl.BlockSpec(memory_space=vmem),
    )(allowed, query, keys, values, kv)


def gather_pipe(piece, order):
    for name in order:
        piece = lax.all_gather(piece, name, axis=0, tiled=True)
    return piece


def on_device(
    x_first, x_second, stale_kv, w_qkv, w_out, q_gain, k_gain, layout, counts, slot_block
):
    me = lax.axis_index(PIPE)
    n_seq = math.prod(s for _, s in SEQ_PARTS)
    tokens = BPM * BLOCK
    heads = w_qkv.shape[2] // HS
    width = heads * HS
    scale = 1.0 / math.sqrt(HS)
    linked = slot_mask(layout, counts, slot_block)
    total_blocks = linked.shape[0]
    block_ids = jnp.arange(total_blocks, dtype=jnp.int32)
    batch_of = block_ids // BPM
    mine = lax.dynamic_slice_in_dim(linked, me * BPM, BPM, 0)
    remote = mine & (batch_of != me)[None, :]

    nz = PIPE_PARTS[1][1]
    shifted = [lax.ppermute(stale_kv, PIPE[1], [(i, (i + m) % nz) for i in range(nz)]) for m in range(1, nz)]
    near = jnp.stack([stale_kv] + shifted)
    pair = jnp.stack([x_first, x_second])
    stale = lax.all_gather(near, PIPE[0], axis=0, tiled=True)
    ny = PIPE_PARTS[0][1]
    from_z = (lax.axis_index(PIPE[1]) - jnp.arange(nz, dtype=jnp.int32)) % nz
    order = (jnp.arange(ny, dtype=jnp.int32)[:, None] * nz + from_z[None, :]).reshape(-1)
    remote_stale = remote[:, order]

    chip = SEQ_PARTS[-1][1]

    def exchange_rows(x):
        steps = x.shape[0]
        spread = jnp.broadcast_to(x[:, None], (steps, n_seq // chip) + x.shape[1:])
        among = lax.all_to_all(spread, SEQ[:-1], 1, 1, tiled=False)
        spread = jnp.broadcast_to(among[:, None], (steps, chip) + among.shape[1:])
        return lax.all_to_all(spread, SEQ[-1], 1, 1, tiled=False).reshape(steps, tokens, -1)

    n_proj = w_qkv.shape[0]
    w_all = w_qkv.transpose(1, 0, 2).reshape(w_qkv.shape[1], n_proj * width)
    xs = exchange_rows(pair)
    raw = jnp.dot(xs.reshape(-1, xs.shape[-1]), w_all, preferred_element_type=jnp.float32)
    raw = raw.reshape(xs.shape[0], tokens, n_proj, width)

    def project(raw):
        query = normalize(raw[:, 0], q_gain, HS).astype(jnp.bfloat16)
        keys = normalize(raw[:, 1], k_gain, HS).astype(jnp.bfloat16)
        values = raw[:, 2].astype(jnp.bfloat16)
        return (query, keys, values)

    q1, k1, v1 = project(raw[0])
    q2, k2, v2 = project(raw[1])

    fresh_kv = gather_pipe(jnp.stack([k1, v1])[None], tuple(reversed(PIPE)))

    def attend(query, keys, values, kv, remote):
        allowed = remote[0].astype(jnp.int32)
        attn = block_attend(allowed, query, keys, values, kv, scale)
        part = jnp.dot(attn, w_out, preferred_element_type=jnp.float32).astype(jnp.bfloat16)
        split = part.reshape(chip, n_seq // chip, tokens // n_seq, -1)
        pair_sum = jnp.sum(lax.all_to_all(split, SEQ[-1], 0, 0, tiled=False).astype(jnp.float32), axis=0)
        sent = lax.all_to_all(pair_sum.astype(jnp.bfloat16), SEQ[:-1], 0, 0, tiled=False)
        return jnp.sum(sent.astype(jnp.float32), axis=0).astype(jnp.bfloat16)

    out_first = attend(q1, k1, v1, stale, remote_stale)
    out_first, fresh_kv = lax.optimization_barrier((out_first, fresh_kv))
    out_second = attend(q2, k2, v2, fresh_kv, remote)
    return (out_first, out_second)


def solution(mesh):
    names = PIPE_PARTS + SEQ_PARTS
    fine = Mesh(
        np.asarray(mesh.devices).reshape([s for _, s in names]), tuple(n for n, _ in names)
    )
    rows = P(PIPE + SEQ, None)
    placed = (
        rows,
        rows,
        P(None, PIPE, SEQ),
        P(None, None, SEQ),
        P(SEQ, None),
        P(SEQ),
        P(SEQ),
        P(),
        P(),
        P(),
    )
    return jax.shard_map(
        on_device,
        mesh=fine,
        in_specs=placed,
        out_specs=(rows, rows),
        check_vma=False,
    )
```

```python
import functools
import math

import jax
import jax.numpy as jnp
import numpy as np
from jax import lax
from jax.experimental import pallas as pl
from jax.experimental.pallas import tpu as pltpu
from jax.sharding import Mesh
from jax.sharding import PartitionSpec as P

HS = 64
BLOCK = 128
BPM = 1


HIGH = lax.Precision.HIGHEST
NEG = -1e30

PIPE_PARTS = (("y", 8), ("zl", 4))
SEQ_PARTS = (("zh", 2), ("x", 4), ("c", 2))
PIPE = tuple(n for n, _ in PIPE_PARTS)
SEQ = tuple(n for n, _ in SEQ_PARTS)


def slot_mask(layout, counts, slot_block):
    total = layout.shape[0]
    width = layout.shape[1]
    blocks = jnp.arange(total, dtype=jnp.int32)
    valid = jnp.arange(width, dtype=jnp.int32)[None, :] < counts[:, None]
    member = jnp.sum(
        ((layout[:, :, None] == blocks[None, None, :]) & valid[:, :, None]).astype(jnp.float32),
        axis=1,
    )
    placed = (slot_block[:, None] == blocks[None, :]).astype(jnp.float32)
    linked = jnp.dot(jnp.dot(placed, member, precision=HIGH), placed.T, precision=HIGH)
    return linked > 0.5


def normalize(raw, gain, size):
    count = raw.shape[0]
    grid = raw.reshape(count, -1, size)
    factor = lax.rsqrt(jnp.mean(grid * grid, axis=2, keepdims=True) + 1e-06)
    return (grid * factor).reshape(count, -1) * gain[None, :]


def attn_kernel(allowed_ref, q_ref, k_ref, v_ref, kv_ref, o_ref, *, scale, n_blocks):
    q = q_ref[...] * jnp.asarray(scale, q_ref.dtype)
    rows, width = q.shape
    lane = lax.broadcasted_iota(jnp.int32, (rows, width), 1)
    zero = jnp.zeros_like(q)
    qt0 = jnp.where(lane < HS, q, zero).T
    qt1 = jnp.where(lane < HS, zero, q).T
    first = lax.broadcasted_iota(jnp.int32, (width, rows), 0) < HS

    def update(carry, kb, vb):
        m0, m1, l0, l1, acc = carry
        s0 = jnp.dot(kb, qt0, preferred_element_type=jnp.float32)
        s1 = jnp.dot(kb, qt1, preferred_element_type=jnp.float32)
        n0 = jnp.maximum(m0, jnp.max(s0, axis=0, keepdims=True))
        n1 = jnp.maximum(m1, jnp.max(s1, axis=0, keepdims=True))
        a0 = jnp.exp(m0 - n0)
        a1 = jnp.exp(m1 - n1)
        p0 = jnp.exp(s0 - n0)
        p1 = jnp.exp(s1 - n1)
        l0 = l0 * a0 + jnp.sum(p0, axis=0, keepdims=True)
        l1 = l1 * a1 + jnp.sum(p1, axis=0, keepdims=True)
        vt = vb.T
        pv0 = jnp.dot(vt, p0.astype(vb.dtype), preferred_element_type=jnp.float32)
        pv1 = jnp.dot(vt, p1.astype(vb.dtype), preferred_element_type=jnp.float32)
        acc = acc * jnp.where(first, a0, a1) + jnp.where(first, pv0, pv1)
        return (n0, n1, l0, l1, acc)

    init = (
        jnp.full((1, rows), NEG, jnp.float32),
        jnp.full((1, rows), NEG, jnp.float32),
        jnp.zeros((1, rows), jnp.float32),
        jnp.zeros((1, rows), jnp.float32),
        jnp.zeros((width, rows), jnp.float32),
    )
    carry = update(init, k_ref[...], v_ref[...])

    def visit(b, carry):
        return update(carry, kv_ref[b, 0], kv_ref[b, 1])

    def body(b, carry):
        return lax.cond(allowed_ref[b] > 0, functools.partial(visit, b), lambda c: c, carry)

    m0, m1, l0, l1, acc = lax.fori_loop(0, n_blocks, body, carry)
    o_ref[...] = (acc / jnp.where(first, l0, l1)).T.astype(o_ref.dtype)


def block_attend(allowed, query, keys, values, kv, scale):
    n_blocks = kv.shape[0]
    vmem = pltpu.MemorySpace.VMEM
    return pl.pallas_call(
        functools.partial(attn_kernel, scale=scale, n_blocks=n_blocks),
        out_shape=jax.ShapeDtypeStruct(query.shape, jnp.bfloat16),
        in_specs=[pl.BlockSpec(memory_space=pltpu.MemorySpace.SMEM)] + [pl.BlockSpec(memory_space=vmem)] * 4,
        out_specs=pl.BlockSpec(memory_space=vmem),
    )(allowed, query, keys, values, kv)


def on_device(
    x_first, x_second, stale_kv, w_qkv, w_out, q_gain, k_gain, layout, counts, slot_block
):
    me = lax.axis_index(PIPE)
    n_seq = math.prod(s for _, s in SEQ_PARTS)
    tokens = BPM * BLOCK
    heads = w_qkv.shape[2] // HS
    width = heads * HS
    scale = 1.0 / math.sqrt(HS)
    linked = slot_mask(layout, counts, slot_block)
    total_blocks = linked.shape[0]
    block_ids = jnp.arange(total_blocks, dtype=jnp.int32)
    batch_of = block_ids // BPM
    mine = lax.dynamic_slice_in_dim(linked, me * BPM, BPM, 0)
    remote = mine & (batch_of != me)[None, :]

    near = lax.all_gather(stale_kv[None], PIPE[1], axis=0, tiled=True)
    first_rows, near = lax.optimization_barrier((x_first, near))
    stale = lax.all_gather(near, PIPE[0], axis=0, tiled=True)

    chip = SEQ_PARTS[-1][1]

    def exchange_rows(x):
        steps = x.shape[0]
        spread = jnp.broadcast_to(x[:, None], (steps, n_seq // chip) + x.shape[1:])
        among = lax.all_to_all(spread, SEQ[:-1], 1, 1, tiled=False)
        spread = jnp.broadcast_to(among[:, None], (steps, chip) + among.shape[1:])
        return lax.all_to_all(spread, SEQ[-1], 1, 1, tiled=False).reshape(steps, tokens, -1)

    n_proj = w_qkv.shape[0]
    w_all = w_qkv.transpose(1, 0, 2).reshape(w_qkv.shape[1], n_proj * width)
    def project(x):
        xs = exchange_rows(x[None])[0]
        raw = jnp.dot(xs, w_all, preferred_element_type=jnp.float32).reshape(tokens, n_proj, width)
        query = normalize(raw[:, 0], q_gain, HS).astype(jnp.bfloat16)
        keys = normalize(raw[:, 1], k_gain, HS).astype(jnp.bfloat16)
        values = raw[:, 2].astype(jnp.bfloat16)
        return (query, keys, values)

    q1, k1, v1 = project(first_rows)

    near_fresh = lax.all_gather(jnp.stack([k1, v1])[None], PIPE[1], axis=0, tiled=True)
    second_rows, near_fresh = lax.optimization_barrier((x_second, near_fresh))
    fresh_kv = lax.all_gather(near_fresh, PIPE[0], axis=0, tiled=True)
    q2, k2, v2 = project(second_rows)

    def attend(query, keys, values, kv, remote):
        allowed = remote[0].astype(jnp.int32)
        attn = block_attend(allowed, query, keys, values, kv, scale)
        part = jnp.dot(attn, w_out, preferred_element_type=jnp.float32).astype(jnp.bfloat16)
        split = part.reshape(chip, n_seq // chip, tokens // n_seq, -1)
        pair_sum = jnp.sum(lax.all_to_all(split, SEQ[-1], 0, 0, tiled=False).astype(jnp.float32), axis=0)
        sent = lax.all_to_all(pair_sum.astype(jnp.bfloat16), SEQ[:-1], 0, 0, tiled=False)
        return jnp.sum(sent.astype(jnp.float32), axis=0).astype(jnp.bfloat16)

    out_first = attend(q1, k1, v1, stale, remote)
    out_first, fresh_kv = lax.optimization_barrier((out_first, fresh_kv))
    out_second = attend(q2, k2, v2, fresh_kv, remote)
    return (out_first, out_second)


def solution(mesh):
    names = PIPE_PARTS + SEQ_PARTS
    fine = Mesh(
        np.asarray(mesh.devices).reshape([s for _, s in names]), tuple(n for n, _ in names)
    )
    rows = P(PIPE + SEQ, None)
    placed = (
        rows,
        rows,
        P(None, PIPE, SEQ),
        P(None, None, SEQ),
        P(SEQ, None),
        P(SEQ),
        P(SEQ),
        P(),
        P(),
        P(),
    )
    return jax.shard_map(
        on_device,
        mesh=fine,
        in_specs=placed,
        out_specs=(rows, rows),
        check_vma=False,
    )
```

```python
import functools
import math

import jax
import jax.numpy as jnp
import numpy as np
from jax import lax
from jax.experimental import pallas as pl
from jax.experimental.pallas import tpu as pltpu
from jax.sharding import Mesh
from jax.sharding import PartitionSpec as P

HS = 64
BLOCK = 128
BPM = 1


HIGH = lax.Precision.HIGHEST
NEG = -1e30

PIPE_PARTS = (("y", 8), ("zl", 4))
SEQ_PARTS = (("zh", 2), ("x", 4), ("c", 2))
PIPE = tuple(n for n, _ in PIPE_PARTS)
SEQ = tuple(n for n, _ in SEQ_PARTS)


def slot_mask(layout, counts, slot_block):
    total = layout.shape[0]
    width = layout.shape[1]
    blocks = jnp.arange(total, dtype=jnp.int32)
    valid = jnp.arange(width, dtype=jnp.int32)[None, :] < counts[:, None]
    member = jnp.sum(
        ((layout[:, :, None] == blocks[None, None, :]) & valid[:, :, None]).astype(jnp.float32),
        axis=1,
    )
    placed = (slot_block[:, None] == blocks[None, :]).astype(jnp.float32)
    linked = jnp.dot(jnp.dot(placed, member, precision=HIGH), placed.T, precision=HIGH)
    return linked > 0.5


def normalize(raw, gain, size):
    count = raw.shape[0]
    grid = raw.reshape(count, -1, size)
    factor = lax.rsqrt(jnp.mean(grid * grid, axis=2, keepdims=True) + 1e-06)
    return (grid * factor).reshape(count, -1) * gain[None, :]


def attn_kernel(allowed_ref, q_ref, k_ref, v_ref, kv_ref, w_ref, o_ref, *, scale, n_blocks):
    q = q_ref[...] * jnp.asarray(scale, q_ref.dtype)
    rows, width = q.shape
    lane = lax.broadcasted_iota(jnp.int32, (rows, width), 1)
    zero = jnp.zeros_like(q)
    qt0 = jnp.where(lane < HS, q, zero).T
    qt1 = jnp.where(lane < HS, zero, q).T
    first = lax.broadcasted_iota(jnp.int32, (width, rows), 0) < HS

    def update(carry, kb, vb):
        m0, m1, l0, l1, acc = carry
        s0 = jnp.dot(kb, qt0, preferred_element_type=jnp.float32)
        s1 = jnp.dot(kb, qt1, preferred_element_type=jnp.float32)
        n0 = jnp.maximum(m0, jnp.max(s0, axis=0, keepdims=True))
        n1 = jnp.maximum(m1, jnp.max(s1, axis=0, keepdims=True))
        a0 = jnp.exp(m0 - n0)
        a1 = jnp.exp(m1 - n1)
        p0 = jnp.exp(s0 - n0)
        p1 = jnp.exp(s1 - n1)
        l0 = l0 * a0 + jnp.sum(p0, axis=0, keepdims=True)
        l1 = l1 * a1 + jnp.sum(p1, axis=0, keepdims=True)
        vt = vb.T
        pv0 = jnp.dot(vt, p0.astype(vb.dtype), preferred_element_type=jnp.float32)
        pv1 = jnp.dot(vt, p1.astype(vb.dtype), preferred_element_type=jnp.float32)
        acc = acc * jnp.where(first, a0, a1) + jnp.where(first, pv0, pv1)
        return (n0, n1, l0, l1, acc)

    init = (
        jnp.full((1, rows), NEG, jnp.float32),
        jnp.full((1, rows), NEG, jnp.float32),
        jnp.zeros((1, rows), jnp.float32),
        jnp.zeros((1, rows), jnp.float32),
        jnp.zeros((width, rows), jnp.float32),
    )
    carry = update(init, k_ref[...], v_ref[...])

    def visit(b, carry):
        return update(carry, kv_ref[b, 0], kv_ref[b, 1])

    def body(b, carry):
        return lax.cond(allowed_ref[b] > 0, functools.partial(visit, b), lambda c: c, carry)

    m0, m1, l0, l1, acc = lax.fori_loop(0, n_blocks, body, carry)
    attn = (acc / jnp.where(first, l0, l1)).T.astype(q_ref.dtype)
    o_ref[...] = jnp.dot(attn, w_ref[...], preferred_element_type=jnp.float32).astype(o_ref.dtype)


def block_attend(allowed, query, keys, values, kv, w_out, scale):
    n_blocks = kv.shape[0]
    vmem = pltpu.MemorySpace.VMEM
    return pl.pallas_call(
        functools.partial(attn_kernel, scale=scale, n_blocks=n_blocks),
        out_shape=jax.ShapeDtypeStruct((query.shape[0], w_out.shape[1]), jnp.bfloat16),
        in_specs=[pl.BlockSpec(memory_space=pltpu.MemorySpace.SMEM)] + [pl.BlockSpec(memory_space=vmem)] * 5,
        out_specs=pl.BlockSpec(memory_space=vmem),
    )(allowed, query, keys, values, kv, w_out)


def gather_pipe(piece, order):
    for name in order:
        piece = lax.all_gather(piece, name, axis=0, tiled=True)
    return piece


def on_device(
    x_first, x_second, stale_kv, w_qkv, w_out, q_gain, k_gain, layout, counts, slot_block
):
    me = lax.axis_index(PIPE)
    n_seq = math.prod(s for _, s in SEQ_PARTS)
    tokens = BPM * BLOCK
    heads = w_qkv.shape[2] // HS
    width = heads * HS
    scale = 1.0 / math.sqrt(HS)
    linked = slot_mask(layout, counts, slot_block)
    total_blocks = linked.shape[0]
    block_ids = jnp.arange(total_blocks, dtype=jnp.int32)
    batch_of = block_ids // BPM
    mine = lax.dynamic_slice_in_dim(linked, me * BPM, BPM, 0)
    remote = mine & (batch_of != me)[None, :]

    near = lax.all_gather(stale_kv[None], PIPE[1], axis=0, tiled=True)
    pair, near = lax.optimization_barrier((jnp.stack([x_first, x_second]), near))
    stale = lax.all_gather(near, PIPE[0], axis=0, tiled=True)

    chip = SEQ_PARTS[-1][1]

    def exchange_rows(x):
        steps = x.shape[0]
        spread = jnp.broadcast_to(x[:, None], (steps, n_seq // chip) + x.shape[1:])
        among = lax.all_to_all(spread, SEQ[:-1], 1, 1, tiled=False)
        spread = jnp.broadcast_to(among[:, None], (steps, chip) + among.shape[1:])
        return lax.all_to_all(spread, SEQ[-1], 1, 1, tiled=False).reshape(steps, tokens, -1)

    n_proj = w_qkv.shape[0]
    w_all = w_qkv.transpose(1, 0, 2).reshape(w_qkv.shape[1], n_proj * width)
    xs = exchange_rows(pair)
    raw = jnp.dot(xs.reshape(-1, xs.shape[-1]), w_all, preferred_element_type=jnp.float32)
    raw = raw.reshape(xs.shape[0], tokens, n_proj, width)

    def project(raw):
        query = normalize(raw[:, 0], q_gain, HS).astype(jnp.bfloat16)
        keys = normalize(raw[:, 1], k_gain, HS).astype(jnp.bfloat16)
        values = raw[:, 2].astype(jnp.bfloat16)
        return (query, keys, values)

    q1, k1, v1 = project(raw[0])
    q2, k2, v2 = project(raw[1])

    fresh_kv = gather_pipe(jnp.stack([k1, v1])[None], tuple(reversed(PIPE)))

    def attend(query, keys, values, kv, remote):
        allowed = remote[0].astype(jnp.int32)
        part = block_attend(allowed, query, keys, values, kv, w_out, scale)
        split = part.reshape(chip, n_seq // chip, tokens // n_seq, -1)
        pair_sum = jnp.sum(lax.all_to_all(split, SEQ[-1], 0, 0, tiled=False).astype(jnp.float32), axis=0)
        sent = lax.all_to_all(pair_sum.astype(jnp.bfloat16), SEQ[:-1], 0, 0, tiled=False)
        return jnp.sum(sent.astype(jnp.float32), axis=0).astype(jnp.bfloat16)

    out_first = attend(q1, k1, v1, stale, remote)
    out_first, fresh_kv = lax.optimization_barrier((out_first, fresh_kv))
    out_second = attend(q2, k2, v2, fresh_kv, remote)
    return (out_first, out_second)


def solution(mesh):
    names = PIPE_PARTS + SEQ_PARTS
    fine = Mesh(
        np.asarray(mesh.devices).reshape([s for _, s in names]), tuple(n for n, _ in names)
    )
    rows = P(PIPE + SEQ, None)
    placed = (
        rows,
        rows,
        P(None, PIPE, SEQ),
        P(None, None, SEQ),
        P(SEQ, None),
        P(SEQ),
        P(SEQ),
        P(),
        P(),
        P(),
    )
    return jax.shard_map(
        on_device,
        mesh=fine,
        in_specs=placed,
        out_specs=(rows, rows),
        check_vma=False,
    )
```

```python
import functools
import math

import jax
import jax.numpy as jnp
import numpy as np
from jax import lax
from jax.experimental import pallas as pl
from jax.experimental.pallas import tpu as pltpu
from jax.sharding import Mesh
from jax.sharding import PartitionSpec as P

HS = 64
BLOCK = 128
BPM = 1


HIGH = lax.Precision.HIGHEST
NEG = -1e30

PIPE_PARTS = (("y", 8), ("zl", 4))
SEQ_PARTS = (("zh", 2), ("x", 4), ("c", 2))
PIPE = tuple(n for n, _ in PIPE_PARTS)
SEQ = tuple(n for n, _ in SEQ_PARTS)


def slot_mask(layout, counts, slot_block):
    total = layout.shape[0]
    width = layout.shape[1]
    blocks = jnp.arange(total, dtype=jnp.int32)
    valid = jnp.arange(width, dtype=jnp.int32)[None, :] < counts[:, None]
    member = jnp.sum(
        ((layout[:, :, None] == blocks[None, None, :]) & valid[:, :, None]).astype(jnp.float32),
        axis=1,
    )
    placed = (slot_block[:, None] == blocks[None, :]).astype(jnp.float32)
    linked = jnp.dot(jnp.dot(placed, member, precision=HIGH), placed.T, precision=HIGH)
    return linked > 0.5


def normalize(raw, gain, size):
    count = raw.shape[0]
    grid = raw.reshape(count, -1, size)
    factor = lax.rsqrt(jnp.mean(grid * grid, axis=2, keepdims=True) + 1e-06)
    return (grid * factor).reshape(count, -1) * gain[None, :]


def attn_kernel(allowed_ref, q_ref, k_ref, v_ref, kv_ref, w_ref, o_ref, *, scale, n_blocks):
    q = q_ref[...] * jnp.asarray(scale, q_ref.dtype)
    rows, width = q.shape
    lane = lax.broadcasted_iota(jnp.int32, (rows, width), 1)
    zero = jnp.zeros_like(q)
    qt0 = jnp.where(lane < HS, q, zero).T
    qt1 = jnp.where(lane < HS, zero, q).T
    first = lax.broadcasted_iota(jnp.int32, (width, rows), 0) < HS

    def update(carry, kb, vb):
        m0, m1, l0, l1, acc = carry
        s0 = jnp.dot(kb, qt0, preferred_element_type=jnp.float32)
        s1 = jnp.dot(kb, qt1, preferred_element_type=jnp.float32)
        n0 = jnp.maximum(m0, jnp.max(s0, axis=0, keepdims=True))
        n1 = jnp.maximum(m1, jnp.max(s1, axis=0, keepdims=True))
        a0 = jnp.exp(m0 - n0)
        a1 = jnp.exp(m1 - n1)
        p0 = jnp.exp(s0 - n0)
        p1 = jnp.exp(s1 - n1)
        l0 = l0 * a0 + jnp.sum(p0, axis=0, keepdims=True)
        l1 = l1 * a1 + jnp.sum(p1, axis=0, keepdims=True)
        vt = vb.T
        pv0 = jnp.dot(vt, p0.astype(vb.dtype), preferred_element_type=jnp.float32)
        pv1 = jnp.dot(vt, p1.astype(vb.dtype), preferred_element_type=jnp.float32)
        acc = acc * jnp.where(first, a0, a1) + jnp.where(first, pv0, pv1)
        return (n0, n1, l0, l1, acc)

    init = (
        jnp.full((1, rows), NEG, jnp.float32),
        jnp.full((1, rows), NEG, jnp.float32),
        jnp.zeros((1, rows), jnp.float32),
        jnp.zeros((1, rows), jnp.float32),
        jnp.zeros((width, rows), jnp.float32),
    )
    carry = update(init, k_ref[...], v_ref[...])

    def visit(b, carry):
        return update(carry, kv_ref[b, 0], kv_ref[b, 1])

    def body(b, carry):
        return lax.cond(allowed_ref[b] > 0, functools.partial(visit, b), lambda c: c, carry)

    m0, m1, l0, l1, acc = lax.fori_loop(0, n_blocks, body, carry)
    attn = (acc / jnp.where(first, l0, l1)).T.astype(q_ref.dtype)
    o_ref[...] = jnp.dot(attn, w_ref[...], preferred_element_type=jnp.float32).astype(o_ref.dtype)


def block_attend(allowed, query, keys, values, kv, w_out, scale):
    n_blocks = kv.shape[0]
    vmem = pltpu.MemorySpace.VMEM
    return pl.pallas_call(
        functools.partial(attn_kernel, scale=scale, n_blocks=n_blocks),
        out_shape=jax.ShapeDtypeStruct((query.shape[0], w_out.shape[1]), jnp.bfloat16),
        in_specs=[pl.BlockSpec(memory_space=pltpu.MemorySpace.SMEM)] + [pl.BlockSpec(memory_space=vmem)] * 5,
        out_specs=pl.BlockSpec(memory_space=vmem),
    )(allowed, query, keys, values, kv, w_out)


def gather_near(piece, name, size):
    spread = jnp.broadcast_to(piece, (size,) + piece.shape[1:])
    return lax.all_to_all(spread, name, 0, 0, tiled=True)


def gather_pipe(piece, order):
    piece = gather_near(piece, order[0], PIPE_PARTS[1][1])
    return lax.all_gather(piece, order[1], axis=0, tiled=True)


def on_device(
    x_first, x_second, stale_kv, w_qkv, w_out, q_gain, k_gain, layout, counts, slot_block
):
    me = lax.axis_index(PIPE)
    n_seq = math.prod(s for _, s in SEQ_PARTS)
    tokens = BPM * BLOCK
    heads = w_qkv.shape[2] // HS
    width = heads * HS
    scale = 1.0 / math.sqrt(HS)
    linked = slot_mask(layout, counts, slot_block)
    total_blocks = linked.shape[0]
    block_ids = jnp.arange(total_blocks, dtype=jnp.int32)
    batch_of = block_ids // BPM
    mine = lax.dynamic_slice_in_dim(linked, me * BPM, BPM, 0)
    remote = mine & (batch_of != me)[None, :]

    near = gather_near(stale_kv[None], PIPE[1], PIPE_PARTS[1][1])
    pair, near = lax.optimization_barrier((jnp.stack([x_first, x_second]), near))
    stale = lax.all_gather(near, PIPE[0], axis=0, tiled=True)

    chip = SEQ_PARTS[-1][1]

    def exchange_rows(x):
        steps = x.shape[0]
        spread = jnp.broadcast_to(x[:, None], (steps, n_seq // chip) + x.shape[1:])
        among = lax.all_to_all(spread, SEQ[:-1], 1, 1, tiled=False)
        spread = jnp.broadcast_to(among[:, None], (steps, chip) + among.shape[1:])
        return lax.all_to_all(spread, SEQ[-1], 1, 1, tiled=False).reshape(steps, tokens, -1)

    n_proj = w_qkv.shape[0]
    w_all = w_qkv.transpose(1, 0, 2).reshape(w_qkv.shape[1], n_proj * width)
    xs = exchange_rows(pair)
    raw = jnp.dot(xs.reshape(-1, xs.shape[-1]), w_all, preferred_element_type=jnp.float32)
    raw = raw.reshape(xs.shape[0], tokens, n_proj, width)

    def project(raw):
        query = normalize(raw[:, 0], q_gain, HS).astype(jnp.bfloat16)
        keys = normalize(raw[:, 1], k_gain, HS).astype(jnp.bfloat16)
        values = raw[:, 2].astype(jnp.bfloat16)
        return (query, keys, values)

    q1, k1, v1 = project(raw[0])
    q2, k2, v2 = project(raw[1])

    fresh_kv = gather_pipe(jnp.stack([k1, v1])[None], tuple(reversed(PIPE)))

    def attend(query, keys, values, kv, remote):
        allowed = remote[0].astype(jnp.int32)
        part = block_attend(allowed, query, keys, values, kv, w_out, scale)
        split = part.reshape(chip, n_seq // chip, tokens // n_seq, -1)
        pair_sum = jnp.sum(lax.all_to_all(split, SEQ[-1], 0, 0, tiled=False).astype(jnp.float32), axis=0)
        sent = lax.all_to_all(pair_sum.astype(jnp.bfloat16), SEQ[:-1], 0, 0, tiled=False)
        return jnp.sum(sent.astype(jnp.float32), axis=0).astype(jnp.bfloat16)

    out_first = attend(q1, k1, v1, stale, remote)
    out_first, fresh_kv = lax.optimization_barrier((out_first, fresh_kv))
    out_second = attend(q2, k2, v2, fresh_kv, remote)
    return (out_first, out_second)


def solution(mesh):
    names = PIPE_PARTS + SEQ_PARTS
    fine = Mesh(
        np.asarray(mesh.devices).reshape([s for _, s in names]), tuple(n for n, _ in names)
    )
    rows = P(PIPE + SEQ, None)
    placed = (
        rows,
        rows,
        P(None, PIPE, SEQ),
        P(None, None, SEQ),
        P(SEQ, None),
        P(SEQ),
        P(SEQ),
        P(),
        P(),
        P(),
    )
    return jax.shard_map(
        on_device,
        mesh=fine,
        in_specs=placed,
        out_specs=(rows, rows),
        check_vma=False,
    )
```
